512 devices in a mesh: band: 16 (over z, core), item: 32 (over x, y).
Axes of the slice: x: 4, y: 8, z: 8, core: 2. Of those that a mesh axis runs over, the one named last changes fastest.
Arguments:
- user_factors: bfloat16 [65536, 256], P(('band', 'item')), may hold values from -1.5 to 1.5
- item_factors: float32 [262144, 256], P(('band', 'item')), may hold values from -1.5 to 1.5
- item_mean: float32 [262144, 256], P(('band', 'item')), may hold values from -1.2 to 1.2
- item_square: float32 [262144, 256], P(('band', 'item')), may hold values from 0.0004 to 0.2
- ratings: bfloat16 [16, 1664, 128, 128], P('band', 'item'), may hold values from -6 to 6
- tile_users: int32 [16, 1664], P('band', 'item'), may hold values from 0 to 15
- tile_items: int32 [16, 1664], P('band', 'item'), may hold values from 0 to 127, as said below
- tile_count: int32 [16, 32], P('band', 'item'), may hold values from 6 to 52, as said below
Outputs:
- user_gradient: float32 [65536, 256], P(('band', 'item'))
- factors_new: float32 [262144, 256], P(('band', 'item'))
- mean_new: float32 [262144, 256], P(('band', 'item'))
- square_new: float32 [262144, 256], P(('band', 'item'))
The draws below stay inside these ranges and needn't reach their ends.
Inputs may be any that keep to these rules, and one draw needn't show every extreme that they name: `tile_count`: slots from the count on carry no interaction; in every draw some device uses all 52 slots. `tile_items`: the slots of one device (occupied or not) name at most 2 distinct item blocks of any one owner, the owner of block j being j // 4; in every draw some owner gets 2 distinct blocks from every device of its range.
All inputs are finite; a program needn't handle non-finite values.
Results may differ from the reference program's by a relative error of at most 0.0052.
Values may be sent and summed in bfloat16 or wider, within the bound.
No kernel may reach another device: no remote copies, remote signals or barrier semaphores. Data moves between devices by JAX's collectives and lax.ppermute only.
A program may use at most 64 MiB of HBM per device.

```python
import math
import jax
import jax.numpy as jnp
from jax import lax

R = 256
TILE = 128
UBLK = 1
TILES = 52
IBLK = 4
CAP = 2
SLAB_BLK = 16
SPAN_BLK = 128
USERS = 65536
ITEMS = 262144
N_BAND = 16
N_ITEM = 32


def tile_layout(key):
    base = jax.random.fold_in(key, 31)
    subkeys = jax.random.split(base, 8)
    devices_all = N_BAND * N_ITEM
    load_level = jax.random.randint(subkeys[0], (devices_all,), 1, 9)
    counts_drawn = jnp.maximum(2, TILES * load_level // 8)
    fullest = jax.random.randint(subkeys[1], (), 0, devices_all)
    counts_drawn = jnp.where(jnp.arange(devices_all) == fullest, TILES, counts_drawn)
    scores = jax.random.randint(subkeys[2], (devices_all, N_ITEM, IBLK), 0, 1 << 20) * IBLK + jnp.arange(IBLK)
    allowed = jnp.argsort(scores, axis=-1, stable=True)[:, :, :CAP]
    owner_pick = jax.random.randint(subkeys[3], (devices_all, TILES), 0, N_ITEM)
    slot_pick = jax.random.randint(subkeys[4], (devices_all, TILES), 0, CAP)
    chosen_owner = jax.random.randint(subkeys[5], (), 0, N_ITEM)
    first_pos = jax.random.randint(subkeys[6], (devices_all,), 0, counts_drawn)
    second_pos = (first_pos + 1 + jax.random.randint(subkeys[7], (devices_all,), 0, counts_drawn - 1)) % counts_drawn
    position = jnp.arange(TILES)[None, :]
    is_first = position == first_pos[:, None]
    is_second = position == second_pos[:, None]
    owner_pick = jnp.where(is_first | is_second, chosen_owner, owner_pick)
    slot_pick = jnp.where(is_first, 0, jnp.where(is_second, 1, slot_pick))
    picked = allowed[jnp.arange(devices_all)[:, None], owner_pick, slot_pick]
    blocks = owner_pick * IBLK + picked
    return (counts_drawn.reshape(N_BAND, N_ITEM).astype(jnp.int32), blocks.reshape(N_BAND, N_ITEM * TILES).astype(jnp.int32))


def draw_tile_count(key, part):
    return tile_layout(key)[0]


def draw_tile_items(key, part):
    return tile_layout(key)[1]


def plant(drawn, rng, least, high):
    longest = drawn.shape.index(max(drawn.shape))
    spots = []
    for shift in (0, 1):
        where = [jax.random.randint(jax.random.fold_in(rng, axis), (), 0, length) for axis, length in enumerate(drawn.shape)]
        where[longest] = (where[longest] + shift) % drawn.shape[longest]
        spots.append(tuple(where))
    return drawn.at[spots[0]].set(least).at[spots[1]].set(high)


def level_of(rng, dims, cuts, smallest, largest):
    factor_of = 1.0
    for dim, parts in cuts:
        heights = jax.random.uniform(jax.random.fold_in(jax.random.fold_in(rng, 6), dim), (parts,), jnp.float32, smallest / len(cuts), largest / len(cuts))
        factor_of = factor_of * jnp.repeat(jnp.exp(heights), dims[dim] // parts).reshape((-1,) + (1,) * (len(dims) - 1 - dim))
    return factor_of


def gaussian(rng, extent, spread, bound, cuts=(), kind=jnp.bfloat16):
    gain = level_of(rng, extent, cuts, -0.22, 0.18) if cuts else 1.0
    entries = jax.random.normal(rng, extent, jnp.float32) * spread * gain
    return jnp.minimum(jnp.maximum(entries, -bound), bound).astype(kind)


def setup_inputs(seed: int = 0) -> dict:
    keys = jax.random.split(jax.random.key(seed), 9)
    return {
        "user_factors": gaussian(keys[0], (USERS, R), 0.25, 1.5, ((0, 512),)),
        "item_factors": gaussian(keys[1], (ITEMS, R), 0.25, 1.5, ((0, 512),), jnp.float32),
        "item_mean": gaussian(keys[2], (ITEMS, R), 0.2, 1.2, ((0, 512),), jnp.float32),
        "item_square": jnp.clip(jnp.exp(math.log(0.2) - 6.214608 * jax.random.uniform(keys[3], (ITEMS, R), jnp.float32) ** level_of(keys[3], (ITEMS, R), ((0, 512),), -0.2, 0.2)), 0.0004, 0.2),
        "ratings": gaussian(keys[4], (N_BAND, N_ITEM * TILES, TILE, TILE), 1.0, 6.0, ((0, 16), (1, 32))),
        "tile_users": plant(jax.random.randint(keys[5], (N_BAND, N_ITEM * TILES), 0, SLAB_BLK), jax.random.fold_in(keys[5], 1), 0, SLAB_BLK - 1).astype(jnp.int32),
        "tile_items": draw_tile_items(jax.random.fold_in(keys[8], 71), 0),
        "tile_count": draw_tile_count(jax.random.fold_in(keys[8], 71), 0),
    }


huber_edge = 1.0
beta_first = 0.9
beta_second = 0.999
learn_rate = 0.05
adam_steps = 10.0
adam_epsilon = 1e-08

def adam_update(factors, moment_old, square_old, gradient):
    moment_new = beta_first * moment_old + (1.0 - beta_first) * gradient
    square_new = beta_second * square_old + (1.0 - beta_second) * gradient * gradient
    moment_hat = moment_new / (1.0 - beta_first ** adam_steps)
    square_hat = square_new / (1.0 - beta_second ** adam_steps)
    factors_new = factors - learn_rate * moment_hat / (jnp.sqrt(square_hat) + adam_epsilon)
    return (factors_new, moment_new, square_new)

def reference(user_factors, item_factors, item_mean, item_square, ratings, tile_users, tile_items, tile_count):
    factor_width = user_factors.shape[1]
    slabs = user_factors.reshape(N_BAND, N_ITEM, UBLK * TILE, factor_width).transpose(1, 0, 2, 3)
    slabs = slabs.reshape(N_ITEM, SLAB_BLK, TILE, factor_width)
    spans = item_factors.astype(jnp.bfloat16).reshape(N_BAND, SPAN_BLK, TILE, factor_width)
    tile_data = ratings.reshape(N_BAND, N_ITEM, TILES, TILE, TILE)
    user_ids = tile_users.reshape(N_BAND, N_ITEM, TILES)
    item_ids = tile_items.reshape(N_BAND, N_ITEM, TILES)

    def visit(carry, device):
        user_total, item_total = carry
        band_index = device // N_ITEM
        item_index = device % N_ITEM
        users_here = user_ids[band_index, item_index]
        items_here = item_ids[band_index, item_index]
        is_valid = jnp.arange(TILES, dtype=jnp.int32) < tile_count[band_index, item_index]
        user_tiles = slabs[item_index][users_here].astype(jnp.float32)
        item_tiles = spans[band_index][items_here].astype(jnp.float32)
        residual = jnp.einsum('tur,tir->tui', user_tiles, item_tiles, precision=lax.Precision.HIGHEST)
        residual = residual - tile_data[band_index, item_index].astype(jnp.float32)
        huber_slope = jnp.where(is_valid[:, None, None], jnp.clip(residual, -huber_edge, huber_edge), 0.0)
        huber_slope = lax.optimization_barrier(huber_slope.astype(jnp.bfloat16)).astype(jnp.float32)
        user_terms = jnp.einsum('tui,tir->tur', huber_slope, item_tiles, precision=lax.Precision.HIGHEST)
        item_terms = jnp.einsum('tui,tur->tir', huber_slope, user_tiles, precision=lax.Precision.HIGHEST)
        user_part = jax.ops.segment_sum(user_terms, users_here, num_segments=SLAB_BLK)
        item_part = jax.ops.segment_sum(item_terms, items_here, num_segments=SPAN_BLK)
        item_part = lax.optimization_barrier(item_part.astype(jnp.bfloat16)).astype(jnp.float32)
        user_total = user_total.at[item_index].add(user_part)
        item_total = item_total.at[band_index].add(item_part)
        return ((user_total, item_total), None)
    user_start = jnp.zeros((N_ITEM, SLAB_BLK, TILE, factor_width), jnp.float32)
    item_start = jnp.zeros((N_BAND, SPAN_BLK, TILE, factor_width), jnp.float32)
    devices_all = jnp.arange(N_BAND * N_ITEM, dtype=jnp.int32)
    (user_total, item_total), unused = lax.scan(visit, (user_start, item_start), devices_all)
    user_gradient = user_total.reshape(N_ITEM, N_BAND, UBLK * TILE, factor_width).transpose(1, 0, 2, 3)
    user_gradient = user_gradient.reshape(USERS, factor_width)
    gradient = item_total.reshape(ITEMS, factor_width)
    factors_new, mean_new, square_new = adam_update(item_factors, item_mean, item_square, gradient)
    return (user_gradient, factors_new, mean_new, square_new)
```

```python
import jax
import jax.numpy as jnp
from jax import lax
from jax.sharding import PartitionSpec as P

CAP = 2


huber_edge = 1.0
beta_first = 0.9
beta_second = 0.999
learn_rate = 0.05
adam_steps = 10.0
adam_epsilon = 1e-08


def adam_update(factors, moment_old, square_old, gradient):
    moment_new = beta_first * moment_old + (1.0 - beta_first) * gradient
    square_new = beta_second * square_old + (1.0 - beta_second) * gradient * gradient
    moment_hat = moment_new / (1.0 - beta_first**adam_steps)
    square_hat = square_new / (1.0 - beta_second**adam_steps)
    factors_new = factors - learn_rate * moment_hat / (jnp.sqrt(square_hat) + adam_epsilon)
    return (factors_new, moment_new, square_new)


def body(
    user_factors, item_factors, item_mean, item_square, ratings, tile_users, tile_items, tile_count
):
    factor_width = user_factors.shape[1]
    tile_edge = ratings.shape[2]
    tile_slots = ratings.shape[1]
    owned_blocks = item_factors.shape[0] // tile_edge
    owners = lax.axis_size("item")
    span_blocks = owned_blocks * owners
    users_here = tile_users[0]
    items_here = tile_items[0]
    is_valid = jnp.arange(tile_slots, dtype=jnp.int32) < tile_count[0, 0]
    bands = lax.axis_size("band")
    slab_blocks = lax.all_to_all(
        jnp.broadcast_to(user_factors[None], (bands,) + user_factors.shape),
        "band", split_axis=0, concat_axis=0, tiled=True,
    ).reshape(-1, tile_edge, factor_width)
    user_tiles = jnp.take(slab_blocks, users_here, axis=0)
    block_hits = (
        items_here[None, :] == jnp.arange(span_blocks, dtype=jnp.int32)[:, None]
    ) & is_valid[None, :]
    touched = jnp.any(block_hits, axis=1).reshape(owners, owned_blocks).astype(jnp.int32)
    slot_rank = jnp.cumsum(touched, axis=1) - touched
    slot_match = (slot_rank[:, :, None] == jnp.arange(CAP, dtype=jnp.int32)[None, None, :]) & (
        touched[:, :, None] == 1
    )
    local_ids = jnp.arange(owned_blocks, dtype=jnp.int32)[None, :, None] + 1
    request = jnp.sum(jnp.where(slot_match, local_ids, 0), axis=1) - 1
    tile_slot = items_here // owned_blocks * CAP + slot_rank.reshape(-1)[items_here]
    whole_table = lax.all_gather(item_factors.astype(jnp.bfloat16), "item", axis=0, tiled=True)
    item_tiles = jnp.take(
        whole_table.reshape(span_blocks, tile_edge, factor_width), items_here, axis=0
    )
    residual = jnp.einsum(
        "tur,tir->tui", user_tiles, item_tiles, preferred_element_type=jnp.float32
    )
    residual = residual - ratings[0].astype(jnp.float32)
    huber_slope = jnp.where(
        is_valid[:, None, None], jnp.clip(residual, -huber_edge, huber_edge), 0.0
    ).astype(jnp.bfloat16)
    user_terms = jnp.einsum(
        "tui,tir->tur", huber_slope, item_tiles, preferred_element_type=jnp.float32
    ).reshape(tile_slots, -1)
    item_terms = jnp.einsum(
        "tui,tur->tir", huber_slope, user_tiles, preferred_element_type=jnp.float32
    ).reshape(tile_slots, -1)
    slot_onehot = (
        (tile_slot[None, :] == jnp.arange(owners * CAP, dtype=jnp.int32)[:, None])
        & is_valid[None, :]
    ).astype(jnp.float32)
    send_rows = jnp.dot(slot_onehot, item_terms, precision=lax.Precision.HIGHEST).astype(
        jnp.bfloat16
    )
    send_rows = send_rows.reshape(owners, CAP, tile_edge * factor_width)
    arrived, arrived_ids = (
        lax.all_to_all(send_rows, "item", split_axis=0, concat_axis=0, tiled=True),
        lax.all_to_all(request, "item", split_axis=0, concat_axis=0, tiled=True),
    )
    owner_onehot = (
        arrived_ids[:, :, None] == jnp.arange(owned_blocks, dtype=jnp.int32)[None, None, :]
    ).astype(jnp.bfloat16)
    gradient = jnp.einsum("nco,ncd->od", owner_onehot, arrived, preferred_element_type=jnp.float32)
    gradient = gradient.reshape(owned_blocks * tile_edge, factor_width)
    factors_new, mean_new, square_new = adam_update(item_factors, item_mean, item_square, gradient)
    row_count = user_factors.shape[0] * lax.axis_size("band")
    block_total = row_count // tile_edge
    block_range = jnp.arange(block_total, dtype=jnp.int32)[:, None]
    wanted = ((users_here[None, :] == block_range) & is_valid[None, :]).astype(jnp.float32)
    user_gradient = lax.psum_scatter(
        jnp.dot(wanted, user_terms, precision=lax.Precision.HIGHEST).reshape(
            row_count, factor_width
        ),
        "band",
        scatter_dimension=0,
        tiled=True,
    )
    return (user_gradient, factors_new, mean_new, square_new)


def solution(mesh):
    in_specs = (
        P(("band", "item"), None),
        P(("band", "item"), None),
        P(("band", "item"), None),
        P(("band", "item"), None),
        P("band", "item", None, None),
        P("band", "item"),
        P("band", "item"),
        P("band", "item"),
    )
    out_specs = (
        P(("band", "item"), None),
        P(("band", "item"), None),
        P(("band", "item"), None),
        P(("band", "item"), None),
    )
    return jax.shard_map(body, mesh=mesh, in_specs=in_specs, out_specs=out_specs, check_vma=False)
```

```python
import jax
import jax.numpy as jnp
from jax import lax
from jax.sharding import PartitionSpec as P
from jax.experimental import pallas as pl
from jax.experimental.pallas import tpu as pltpu

CAP = 2


huber_edge = 1.0
beta_first = 0.9
beta_second = 0.999
learn_rate = 0.05
adam_steps = 10.0
adam_epsilon = 1e-08


def adam_update(factors, moment_old, square_old, gradient):
    moment_new = beta_first * moment_old + (1.0 - beta_first) * gradient
    square_new = beta_second * square_old + (1.0 - beta_second) * gradient * gradient
    moment_hat = moment_new / (1.0 - beta_first**adam_steps)
    square_hat = square_new / (1.0 - beta_second**adam_steps)
    factors_new = factors - learn_rate * moment_hat / (jnp.sqrt(square_hat) + adam_epsilon)
    return (factors_new, moment_new, square_new)


def _tile_kernel(users_ref, items_ref, slots_ref, count_ref, slab_ref, table_ref, ratings_ref, user_out, send_out, acc_ref):
    user_out[...] = jnp.zeros(user_out.shape, user_out.dtype)
    acc_ref[...] = jnp.zeros(acc_ref.shape, acc_ref.dtype)
    count = count_ref[0]

    def step(t, carry):
        u = users_ref[t]
        j = items_ref[t]
        s = slots_ref[t]
        user_tile = slab_ref[u]
        item_tile = table_ref[j]
        residual = lax.dot_general(user_tile, item_tile, (((1,), (1,)), ((), ())), preferred_element_type=jnp.float32)
        residual = residual - ratings_ref[t].astype(jnp.float32)
        slope = jnp.where(t < count, jnp.clip(residual, -1.0, 1.0), 0.0)
        user_out[u] += jnp.dot(slope.astype(jnp.bfloat16), item_tile, preferred_element_type=jnp.float32)
        acc_ref[s] += jnp.dot(slope.T.astype(jnp.bfloat16), user_tile, preferred_element_type=jnp.float32)
        return carry

    lax.fori_loop(0, ratings_ref.shape[0], step, 0, unroll=4)
    send_out[...] = acc_ref[...].astype(send_out.dtype)


def tile_work(users, items, slots, count, slab, table, ratings, n_slots, interpret=False):
    vmem = pltpu.MemorySpace.VMEM if hasattr(pltpu, "MemorySpace") else pltpu.VMEM
    edge, width = slab.shape[1], slab.shape[2]
    return pl.pallas_call(
        _tile_kernel,
        grid_spec=pltpu.PrefetchScalarGridSpec(
            num_scalar_prefetch=4,
            grid=(1,),
            in_specs=[pl.BlockSpec(memory_space=vmem)] * 3,
            out_specs=[pl.BlockSpec(memory_space=vmem)] * 2,
            scratch_shapes=[pltpu.VMEM((n_slots, edge, width), jnp.float32)],
        ),
        out_shape=[
            jax.ShapeDtypeStruct(slab.shape, jnp.float32),
            jax.ShapeDtypeStruct((n_slots, edge, width), jnp.bfloat16),
        ],
        compiler_params=pltpu.CompilerParams(vmem_limit_bytes=56 * 1024 * 1024),
        interpret=interpret,
    )(users, items, slots, count, slab, table, ratings)


def body(
    user_factors, item_factors, item_mean, item_square, ratings, tile_users, tile_items, tile_count
):
    factor_width = user_factors.shape[1]
    tile_edge = ratings.shape[2]
    tile_slots = ratings.shape[1]
    owned_blocks = item_factors.shape[0] // tile_edge
    owners = lax.axis_size("item")
    span_blocks = owned_blocks * owners
    users_here = tile_users[0]
    items_here = tile_items[0]
    is_valid = jnp.arange(tile_slots, dtype=jnp.int32) < tile_count[0, 0]
    bands = lax.axis_size("band")
    slab_blocks = lax.all_to_all(
        jnp.broadcast_to(user_factors[None], (bands,) + user_factors.shape),
        "band", split_axis=0, concat_axis=0, tiled=True,
    ).reshape(-1, tile_edge, factor_width)
    block_hits = (
        items_here[None, :] == jnp.arange(span_blocks, dtype=jnp.int32)[:, None]
    ) & is_valid[None, :]
    touched = jnp.any(block_hits, axis=1).reshape(owners, owned_blocks).astype(jnp.int32)
    slot_rank = jnp.cumsum(touched, axis=1) - touched
    slot_match = (slot_rank[:, :, None] == jnp.arange(CAP, dtype=jnp.int32)[None, None, :]) & (
        touched[:, :, None] == 1
    )
    local_ids = jnp.arange(owned_blocks, dtype=jnp.int32)[None, :, None] + 1
    request = jnp.sum(jnp.where(slot_match, local_ids, 0), axis=1) - 1
    tile_slot = items_here // owned_blocks * CAP + slot_rank.reshape(-1)[items_here]
    whole_table = lax.all_gather(item_factors.astype(jnp.bfloat16), "item", axis=0, tiled=True)
    n_slots = owners * CAP
    tile_slot = jnp.clip(tile_slot, 0, n_slots - 1).astype(jnp.int32)
    user_total, send_rows = tile_work(
        jnp.clip(users_here, 0, slab_blocks.shape[0] - 1).astype(jnp.int32),
        jnp.clip(items_here, 0, span_blocks - 1).astype(jnp.int32),
        tile_slot,
        tile_count[0].astype(jnp.int32),
        slab_blocks,
        whole_table.reshape(span_blocks, tile_edge, factor_width),
        ratings[0],
        n_slots,
    )
    send_rows = send_rows.reshape(owners, CAP * tile_edge, factor_width)
    arrived, arrived_ids = (
        lax.all_to_all(send_rows, "item", split_axis=0, concat_axis=0, tiled=True),
        lax.all_to_all(request, "item", split_axis=0, concat_axis=0, tiled=True),
    )
    owner_onehot = (
        arrived_ids[:, :, None] == jnp.arange(owned_blocks, dtype=jnp.int32)[None, None, :]
    ).astype(jnp.bfloat16)
    arrived = arrived.reshape(owners, CAP, tile_edge * factor_width)
    gradient = jnp.einsum("nco,ncd->od", owner_onehot, arrived, preferred_element_type=jnp.float32)
    gradient = gradient.reshape(owned_blocks * tile_edge, factor_width)
    factors_new, mean_new, square_new = adam_update(item_factors, item_mean, item_square, gradient)
    user_gradient = lax.psum_scatter(
        user_total.reshape(-1, factor_width),
        "band",
        scatter_dimension=0,
        tiled=True,
    )
    return (user_gradient, factors_new, mean_new, square_new)


def solution(mesh):
    in_specs = (
        P(("band", "item"), None),
        P(("band", "item"), None),
        P(("band", "item"), None),
        P(("band", "item"), None),
        P("band", "item", None, None),
        P("band", "item"),
        P("band", "item"),
        P("band", "item"),
    )
    out_specs = (
        P(("band", "item"), None),
        P(("band", "item"), None),
        P(("band", "item"), None),
        P(("band", "item"), None),
    )
    return jax.shard_map(body, mesh=mesh, in_specs=in_specs, out_specs=out_specs, check_vma=False)
```

```python
import jax
import jax.numpy as jnp
from jax import lax
from jax.sharding import PartitionSpec as P
from jax.experimental import pallas as pl
from jax.experimental.pallas import tpu as pltpu

CAP = 2


huber_edge = 1.0
beta_first = 0.9
beta_second = 0.999
learn_rate = 0.05
adam_steps = 10.0
adam_epsilon = 1e-08


def adam_update(factors, moment_old, square_old, gradient):
    moment_new = beta_first * moment_old + (1.0 - beta_first) * gradient
    square_new = beta_second * square_old + (1.0 - beta_second) * gradient * gradient
    moment_hat = moment_new / (1.0 - beta_first**adam_steps)
    square_hat = square_new / (1.0 - beta_second**adam_steps)
    factors_new = factors - learn_rate * moment_hat / (jnp.sqrt(square_hat) + adam_epsilon)
    return (factors_new, moment_new, square_new)


def _tile_kernel(users_ref, main_ref, side_ref, slots_ref, count_ref, slab_ref, table_ref, extra_ref, ratings_ref, user_out, send_out, acc_ref):
    user_out[...] = jnp.zeros(user_out.shape, user_out.dtype)
    acc_ref[...] = jnp.zeros(acc_ref.shape, acc_ref.dtype)
    count = count_ref[0]

    def step(t, carry):
        u = users_ref[t]
        j = main_ref[t]
        k = side_ref[t]
        s = slots_ref[t]
        user_tile = slab_ref[u]
        item_tile = jnp.where(k >= 0, extra_ref[jnp.maximum(k, 0)], table_ref[j])
        residual = lax.dot_general(user_tile, item_tile, (((1,), (1,)), ((), ())), preferred_element_type=jnp.float32)
        residual = residual - ratings_ref[t].astype(jnp.float32)
        slope = jnp.where(t < count, jnp.clip(residual, -1.0, 1.0), 0.0)
        user_out[u] += jnp.dot(slope.astype(jnp.bfloat16), item_tile, preferred_element_type=jnp.float32)
        acc_ref[s] += jnp.dot(slope.T.astype(jnp.bfloat16), user_tile, preferred_element_type=jnp.float32)
        return carry

    lax.fori_loop(0, ratings_ref.shape[0], step, 0, unroll=4)
    send_out[...] = acc_ref[...].astype(send_out.dtype)


def tile_work(users, main, side, slots, count, slab, table, extra, ratings, n_slots, interpret=False):
    vmem = pltpu.MemorySpace.VMEM if hasattr(pltpu, "MemorySpace") else pltpu.VMEM
    edge, width = slab.shape[1], slab.shape[2]
    return pl.pallas_call(
        _tile_kernel,
        grid_spec=pltpu.PrefetchScalarGridSpec(
            num_scalar_prefetch=5,
            grid=(1,),
            in_specs=[pl.BlockSpec(memory_space=vmem)] * 4,
            out_specs=[pl.BlockSpec(memory_space=vmem)] * 2,
            scratch_shapes=[pltpu.VMEM((n_slots, edge, width), jnp.float32)],
        ),
        out_shape=[
            jax.ShapeDtypeStruct(slab.shape, jnp.float32),
            jax.ShapeDtypeStruct((n_slots, edge, width), jnp.bfloat16),
        ],
        compiler_params=pltpu.CompilerParams(vmem_limit_bytes=56 * 1024 * 1024),
        interpret=interpret,
    )(users, main, side, slots, count, slab, table, extra, ratings)


def body(
    user_factors, item_factors, item_mean, item_square, ratings, tile_users, tile_items, tile_count
):
    factor_width = user_factors.shape[1]
    tile_edge = ratings.shape[2]
    tile_slots = ratings.shape[1]
    owned_blocks = item_factors.shape[0] // tile_edge
    owners = lax.axis_size("item")
    span_blocks = owned_blocks * owners
    users_here = tile_users[0]
    items_here = tile_items[0]
    is_valid = jnp.arange(tile_slots, dtype=jnp.int32) < tile_count[0, 0]
    bands = lax.axis_size("band")
    slab_blocks = lax.all_to_all(
        jnp.broadcast_to(user_factors[None], (bands,) + user_factors.shape),
        "band", split_axis=0, concat_axis=0, tiled=True,
    ).reshape(-1, tile_edge, factor_width)
    block_hits = (
        items_here[None, :] == jnp.arange(span_blocks, dtype=jnp.int32)[:, None]
    ) & is_valid[None, :]
    touched = jnp.any(block_hits, axis=1).reshape(owners, owned_blocks).astype(jnp.int32)
    slot_rank = jnp.cumsum(touched, axis=1) - touched
    slot_match = (slot_rank[:, :, None] == jnp.arange(CAP, dtype=jnp.int32)[None, None, :]) & (
        touched[:, :, None] == 1
    )
    local_ids = jnp.arange(owned_blocks, dtype=jnp.int32)[None, :, None] + 1
    request = jnp.sum(jnp.where(slot_match, local_ids, 0), axis=1) - 1
    tile_slot = items_here // owned_blocks * CAP + slot_rank.reshape(-1)[items_here]
    own_bf16 = item_factors.astype(jnp.bfloat16).reshape(owned_blocks, tile_edge, factor_width)
    gathered_blocks = owned_blocks - 1
    main_table = lax.all_gather(own_bf16[:gathered_blocks], "item", axis=0, tiled=True)
    extra_table = lax.all_to_all(
        jnp.broadcast_to(own_bf16[gathered_blocks:], (owners, tile_edge, factor_width)),
        "item", split_axis=0, concat_axis=0, tiled=True,
    )
    items_safe = jnp.clip(items_here, 0, span_blocks - 1).astype(jnp.int32)
    item_owner = items_safe // owned_blocks
    item_local = items_safe % owned_blocks
    main_index = item_owner * gathered_blocks + jnp.minimum(item_local, gathered_blocks - 1)
    side_index = jnp.where(item_local >= gathered_blocks, item_owner, -1).astype(jnp.int32)
    n_slots = owners * CAP
    tile_slot = jnp.clip(tile_slot, 0, n_slots - 1).astype(jnp.int32)
    user_total, send_rows = tile_work(
        jnp.clip(users_here, 0, slab_blocks.shape[0] - 1).astype(jnp.int32),
        main_index.astype(jnp.int32),
        side_index,
        tile_slot,
        tile_count[0].astype(jnp.int32),
        slab_blocks,
        main_table,
        extra_table,
        ratings[0],
        n_slots,
    )
    send_rows = send_rows.reshape(owners, CAP * tile_edge, factor_width)
    arrived, arrived_ids = (
        lax.all_to_all(send_rows, "item", split_axis=0, concat_axis=0, tiled=True),
        lax.all_to_all(request, "item", split_axis=0, concat_axis=0, tiled=True),
    )
    owner_onehot = (
        arrived_ids[:, :, None] == jnp.arange(owned_blocks, dtype=jnp.int32)[None, None, :]
    ).astype(jnp.bfloat16)
    arrived = arrived.reshape(owners, CAP, tile_edge * factor_width)
    gradient = jnp.einsum("nco,ncd->od", owner_onehot, arrived, preferred_element_type=jnp.float32)
    gradient = gradient.reshape(owned_blocks * tile_edge, factor_width)
    factors_new, mean_new, square_new = adam_update(item_factors, item_mean, item_square, gradient)
    user_gradient = lax.psum_scatter(
        user_total.reshape(-1, factor_width),
        "band",
        scatter_dimension=0,
        tiled=True,
    )
    return (user_gradient, factors_new, mean_new, square_new)


def solution(mesh):
    in_specs = (
        P(("band", "item"), None),
        P(("band", "item"), None),
        P(("band", "item"), None),
        P(("band", "item"), None),
        P("band", "item", None, None),
        P("band", "item"),
        P("band", "item"),
        P("band", "item"),
    )
    out_specs = (
        P(("band", "item"), None),
        P(("band", "item"), None),
        P(("band", "item"), None),
        P(("band", "item"), None),
    )
    return jax.shard_map(body, mesh=mesh, in_specs=in_specs, out_specs=out_specs, check_vma=False)
```

```python
import jax
import jax.numpy as jnp
from jax import lax
from jax.sharding import PartitionSpec as P
from jax.experimental import pallas as pl
from jax.experimental.pallas import tpu as pltpu

CAP = 2


huber_edge = 1.0
beta_first = 0.9
beta_second = 0.999
learn_rate = 0.05
adam_steps = 10.0
adam_epsilon = 1e-08


def adam_update(factors, moment_old, square_old, gradient):
    moment_new = beta_first * moment_old + (1.0 - beta_first) * gradient
    square_new = beta_second * square_old + (1.0 - beta_second) * gradient * gradient
    moment_hat = moment_new / (1.0 - beta_first**adam_steps)
    square_hat = square_new / (1.0 - beta_second**adam_steps)
    factors_new = factors - learn_rate * moment_hat / (jnp.sqrt(square_hat) + adam_epsilon)
    return (factors_new, moment_new, square_new)


def _tile_kernel(users_ref, items_ref, slots_ref, count_ref, slab_ref, table_ref, ratings_ref, user_out, send_out, acc_ref):
    user_out[...] = jnp.zeros(user_out.shape, user_out.dtype)
    acc_ref[...] = jnp.zeros(acc_ref.shape, acc_ref.dtype)
    count = count_ref[0]

    def step(t, carry):
        u = users_ref[t]
        j = items_ref[t]
        s = slots_ref[t]
        user_tile = slab_ref[u]
        item_tile = table_ref[j]
        residual = lax.dot_general(user_tile, item_tile, (((1,), (1,)), ((), ())), preferred_element_type=jnp.float32)
        residual = residual - ratings_ref[t].astype(jnp.float32)
        slope = jnp.where(t < count, jnp.clip(residual, -1.0, 1.0), 0.0)
        user_out[u] += jnp.dot(slope.astype(jnp.bfloat16), item_tile, preferred_element_type=jnp.float32)
        acc_ref[s] += jnp.dot(slope.T.astype(jnp.bfloat16), user_tile, preferred_element_type=jnp.float32)
        return carry

    lax.fori_loop(0, ratings_ref.shape[0], step, 0, unroll=4)
    send_out[...] = acc_ref[...].astype(send_out.dtype)


def tile_work(users, items, slots, count, slab, table, ratings, n_slots, interpret=False):
    vmem = pltpu.MemorySpace.VMEM if hasattr(pltpu, "MemorySpace") else pltpu.VMEM
    edge, width = slab.shape[1], slab.shape[2]
    return pl.pallas_call(
        _tile_kernel,
        grid_spec=pltpu.PrefetchScalarGridSpec(
            num_scalar_prefetch=4,
            grid=(1,),
            in_specs=[pl.BlockSpec(memory_space=vmem)] * 3,
            out_specs=[pl.BlockSpec(memory_space=vmem)] * 2,
            scratch_shapes=[pltpu.VMEM((n_slots, edge, width), jnp.float32)],
        ),
        out_shape=[
            jax.ShapeDtypeStruct(slab.shape, jnp.float32),
            jax.ShapeDtypeStruct((n_slots, edge, width), jnp.bfloat16),
        ],
        compiler_params=pltpu.CompilerParams(vmem_limit_bytes=56 * 1024 * 1024),
        interpret=interpret,
    )(users, items, slots, count, slab, table, ratings)


def _owner_kernel(ids_ref, arrived_ref, factors_ref, mean_ref, square_ref, factors_out, mean_out, square_out, acc_ref):
    acc_ref[...] = jnp.zeros(acc_ref.shape, acc_ref.dtype)
    edge = arrived_ref.shape[1]
    owned = acc_ref.shape[0] // edge

    def step(r, carry):
        block = ids_ref[r]
        rows = arrived_ref[r].astype(jnp.float32)
        start = pl.multiple_of(jnp.clip(block, 0, owned - 1) * edge, edge)
        acc_ref[pl.ds(start, edge), :] += jnp.where(block >= 0, rows, 0.0)
        return carry

    lax.fori_loop(0, arrived_ref.shape[0], step, 0, unroll=4)
    factors_new, mean_new, square_new = adam_update(factors_ref[...], mean_ref[...], square_ref[...], acc_ref[...])
    factors_out[...] = factors_new
    mean_out[...] = mean_new
    square_out[...] = square_new


def owner_update(ids, arrived, factors, mean, square, interpret=False):
    vmem = pltpu.MemorySpace.VMEM if hasattr(pltpu, "MemorySpace") else pltpu.VMEM
    out = jax.ShapeDtypeStruct(factors.shape, jnp.float32)
    return pl.pallas_call(
        _owner_kernel,
        grid_spec=pltpu.PrefetchScalarGridSpec(
            num_scalar_prefetch=1,
            grid=(1,),
            in_specs=[pl.BlockSpec(memory_space=vmem)] * 4,
            out_specs=[pl.BlockSpec(memory_space=vmem)] * 3,
            scratch_shapes=[pltpu.VMEM(factors.shape, jnp.float32)],
        ),
        out_shape=[out, out, out],
        compiler_params=pltpu.CompilerParams(vmem_limit_bytes=48 * 1024 * 1024),
        interpret=interpret,
    )(ids, arrived, factors, mean, square)


def body(
    user_factors, item_factors, item_mean, item_square, ratings, tile_users, tile_items, tile_count
):
    factor_width = user_factors.shape[1]
    tile_edge = ratings.shape[2]
    tile_slots = ratings.shape[1]
    owned_blocks = item_factors.shape[0] // tile_edge
    owners = lax.axis_size("item")
    span_blocks = owned_blocks * owners
    users_here = tile_users[0]
    items_here = tile_items[0]
    is_valid = jnp.arange(tile_slots, dtype=jnp.int32) < tile_count[0, 0]
    bands = lax.axis_size("band")
    slab_blocks = lax.all_to_all(
        jnp.broadcast_to(user_factors[None], (bands,) + user_factors.shape),
        "band", split_axis=0, concat_axis=0, tiled=True,
    ).reshape(-1, tile_edge, factor_width)
    block_hits = (
        items_here[None, :] == jnp.arange(span_blocks, dtype=jnp.int32)[:, None]
    ) & is_valid[None, :]
    touched = jnp.any(block_hits, axis=1).reshape(owners, owned_blocks).astype(jnp.int32)
    slot_rank = jnp.cumsum(touched, axis=1) - touched
    slot_match = (slot_rank[:, :, None] == jnp.arange(CAP, dtype=jnp.int32)[None, None, :]) & (
        touched[:, :, None] == 1
    )
    local_ids = jnp.arange(owned_blocks, dtype=jnp.int32)[None, :, None] + 1
    request = jnp.sum(jnp.where(slot_match, local_ids, 0), axis=1) - 1
    tile_slot = items_here // owned_blocks * CAP + slot_rank.reshape(-1)[items_here]
    whole_table = lax.all_gather(item_factors.astype(jnp.bfloat16), "item", axis=0, tiled=True)
    n_slots = owners * CAP
    tile_slot = jnp.clip(tile_slot, 0, n_slots - 1).astype(jnp.int32)
    user_total, send_rows = tile_work(
        jnp.clip(users_here, 0, slab_blocks.shape[0] - 1).astype(jnp.int32),
        jnp.clip(items_here, 0, span_blocks - 1).astype(jnp.int32),
        tile_slot,
        tile_count[0].astype(jnp.int32),
        slab_blocks,
        whole_table.reshape(span_blocks, tile_edge, factor_width),
        ratings[0],
        n_slots,
    )
    send_rows = send_rows.reshape(owners, CAP * tile_edge, factor_width)
    arrived, arrived_ids = (
        lax.all_to_all(send_rows, "item", split_axis=0, concat_axis=0, tiled=True),
        lax.all_to_all(request, "item", split_axis=0, concat_axis=0, tiled=True),
    )
    factors_new, mean_new, square_new = owner_update(
        arrived_ids.reshape(-1).astype(jnp.int32),
        arrived.reshape(owners * CAP, tile_edge, factor_width),
        item_factors,
        item_mean,
        item_square,
    )
    user_gradient = lax.psum_scatter(
        user_total.reshape(-1, factor_width),
        "band",
        scatter_dimension=0,
        tiled=True,
    )
    return (user_gradient, factors_new, mean_new, square_new)


def solution(mesh):
    in_specs = (
        P(("band", "item"), None),
        P(("band", "item"), None),
        P(("band", "item"), None),
        P(("band", "item"), None),
        P("band", "item", None, None),
        P("band", "item"),
        P("band", "item"),
        P("band", "item"),
    )
    out_specs = (
        P(("band", "item"), None),
        P(("band", "item"), None),
        P(("band", "item"), None),
        P(("band", "item"), None),
    )
    return jax.shard_map(body, mesh=mesh, in_specs=in_specs, out_specs=out_specs, check_vma=False)
```

```python
import jax
import jax.numpy as jnp
from jax import lax
from jax.sharding import PartitionSpec as P
from jax.experimental import pallas as pl
from jax.experimental.pallas import tpu as pltpu

CAP = 2


huber_edge = 1.0
beta_first = 0.9
beta_second = 0.999
learn_rate = 0.05
adam_steps = 10.0
adam_epsilon = 1e-08


def adam_update(factors, moment_old, square_old, gradient):
    moment_new = beta_first * moment_old + (1.0 - beta_first) * gradient
    square_new = beta_second * square_old + (1.0 - beta_second) * gradient * gradient
    moment_hat = moment_new / (1.0 - beta_first**adam_steps)
    square_hat = square_new / (1.0 - beta_second**adam_steps)
    factors_new = factors - learn_rate * moment_hat / (jnp.sqrt(square_hat) + adam_epsilon)
    return (factors_new, moment_new, square_new)


def _tile_kernel(users_ref, items_ref, slots_ref, first_ref, count_ref, slab_ref, table_hbm, ratings_ref, user_out, send_out, acc_ref, item_buf, sem):
    user_out[...] = jnp.zeros(user_out.shape, user_out.dtype)
    count = count_ref[0]
    n_tiles = ratings_ref.shape[0]

    def fetch(t, slot):
        return pltpu.make_async_copy(table_hbm.at[items_ref[t]], item_buf.at[slot], sem.at[slot])

    fetch(0, 0).start()

    def step(t, carry):
        slot = t % 2

        @pl.when(t + 1 < n_tiles)
        def _():
            fetch(t + 1, 1 - slot).start()

        fetch(t, slot).wait()
        u = users_ref[t]
        s = slots_ref[t]
        user_tile = slab_ref[u]
        item_tile = item_buf[slot]
        residual = lax.dot_general(user_tile, item_tile, (((1,), (1,)), ((), ())), preferred_element_type=jnp.float32)
        residual = residual - ratings_ref[t].astype(jnp.float32)
        slope = jnp.where(t < count, jnp.clip(residual, -1.0, 1.0), 0.0)
        user_out[u] += jnp.dot(slope.astype(jnp.bfloat16), item_tile, preferred_element_type=jnp.float32)
        fresh = jnp.dot(slope.T.astype(jnp.bfloat16), user_tile, preferred_element_type=jnp.float32)
        acc_ref[s] = jnp.where(first_ref[t] > 0, fresh, acc_ref[s] + fresh)
        return carry

    lax.fori_loop(0, n_tiles, step, 0, unroll=4)
    send_out[...] = acc_ref[...].astype(send_out.dtype)


def tile_work(users, items, slots, first, count, slab, table, ratings, n_slots, interpret=False):
    vmem = pltpu.MemorySpace.VMEM if hasattr(pltpu, "MemorySpace") else pltpu.VMEM
    edge, width = slab.shape[1], slab.shape[2]
    return pl.pallas_call(
        _tile_kernel,
        grid_spec=pltpu.PrefetchScalarGridSpec(
            num_scalar_prefetch=5,
            grid=(1,),
            in_specs=[
                pl.BlockSpec(memory_space=vmem),
                pl.BlockSpec(memory_space=pl.ANY),
                pl.BlockSpec(memory_space=vmem),
            ],
            out_specs=[pl.BlockSpec(memory_space=vmem)] * 2,
            scratch_shapes=[
                pltpu.VMEM((n_slots, edge, width), jnp.float32),
                pltpu.VMEM((2, edge, width), table.dtype),
                pltpu.SemaphoreType.DMA((2,)),
            ],
        ),
        out_shape=[
            jax.ShapeDtypeStruct(slab.shape, jnp.float32),
            jax.ShapeDtypeStruct((n_slots, edge, width), jnp.bfloat16),
        ],
        compiler_params=pltpu.CompilerParams(vmem_limit_bytes=48 * 1024 * 1024),
        interpret=interpret,
    )(users, items, slots, first, count, slab, table, ratings)


def _owner_kernel(ids_ref, arrived_ref, factors_ref, mean_ref, square_ref, factors_out, mean_out, square_out, acc_ref):
    acc_ref[...] = jnp.zeros(acc_ref.shape, acc_ref.dtype)
    edge = arrived_ref.shape[1]
    owned = acc_ref.shape[0] // edge

    def step(r, carry):
        block = ids_ref[r]
        rows = arrived_ref[r].astype(jnp.float32)
        start = pl.multiple_of(jnp.clip(block, 0, owned - 1) * edge, edge)
        acc_ref[pl.ds(start, edge), :] += jnp.where(block >= 0, rows, 0.0)
        return carry

    lax.fori_loop(0, arrived_ref.shape[0], step, 0, unroll=4)
    factors_new, mean_new, square_new = adam_update(factors_ref[...], mean_ref[...], square_ref[...], acc_ref[...])
    factors_out[...] = factors_new
    mean_out[...] = mean_new
    square_out[...] = square_new


def owner_update(ids, arrived, factors, mean, square, interpret=False):
    vmem = pltpu.MemorySpace.VMEM if hasattr(pltpu, "MemorySpace") else pltpu.VMEM
    out = jax.ShapeDtypeStruct(factors.shape, jnp.float32)
    return pl.pallas_call(
        _owner_kernel,
        grid_spec=pltpu.PrefetchScalarGridSpec(
            num_scalar_prefetch=1,
            grid=(1,),
            in_specs=[pl.BlockSpec(memory_space=vmem)] * 4,
            out_specs=[pl.BlockSpec(memory_space=vmem)] * 3,
            scratch_shapes=[pltpu.VMEM(factors.shape, jnp.float32)],
        ),
        out_shape=[out, out, out],
        compiler_params=pltpu.CompilerParams(vmem_limit_bytes=48 * 1024 * 1024),
        interpret=interpret,
    )(ids, arrived, factors, mean, square)


def body(
    user_factors, item_factors, item_mean, item_square, ratings, tile_users, tile_items, tile_count
):
    factor_width = user_factors.shape[1]
    tile_edge = ratings.shape[2]
    tile_slots = ratings.shape[1]
    owned_blocks = item_factors.shape[0] // tile_edge
    owners = lax.axis_size("item")
    span_blocks = owned_blocks * owners
    users_here = tile_users[0]
    items_here = tile_items[0]
    is_valid = jnp.arange(tile_slots, dtype=jnp.int32) < tile_count[0, 0]
    bands = lax.axis_size("band")
    slab_blocks = lax.all_to_all(
        jnp.broadcast_to(user_factors[None], (bands,) + user_factors.shape),
        "band", split_axis=0, concat_axis=0, tiled=True,
    ).reshape(-1, tile_edge, factor_width)
    block_hits = (
        items_here[None, :] == jnp.arange(span_blocks, dtype=jnp.int32)[:, None]
    ) & is_valid[None, :]
    touched = jnp.any(block_hits, axis=1).reshape(owners, owned_blocks).astype(jnp.int32)
    slot_rank = jnp.cumsum(touched, axis=1) - touched
    slot_match = (slot_rank[:, :, None] == jnp.arange(CAP, dtype=jnp.int32)[None, None, :]) & (
        touched[:, :, None] == 1
    )
    local_ids = jnp.arange(owned_blocks, dtype=jnp.int32)[None, :, None] + 1
    request = jnp.sum(jnp.where(slot_match, local_ids, 0), axis=1) - 1
    tile_slot = items_here // owned_blocks * CAP + slot_rank.reshape(-1)[items_here]
    whole_table = lax.all_gather(item_factors.astype(jnp.bfloat16), "item", axis=0, tiled=True)
    n_slots = owners * CAP
    tile_slot = jnp.clip(tile_slot, 0, n_slots - 1).astype(jnp.int32)
    slot_order = jnp.arange(tile_slots, dtype=jnp.int32)
    seen_before = (tile_slot[None, :] == tile_slot[:, None]) & (slot_order[None, :] < slot_order[:, None])
    first_touch = jnp.logical_not(jnp.any(seen_before, axis=1)).astype(jnp.int32)
    user_total, send_rows = tile_work(
        jnp.clip(users_here, 0, slab_blocks.shape[0] - 1).astype(jnp.int32),
        jnp.clip(items_here, 0, span_blocks - 1).astype(jnp.int32),
        tile_slot,
        first_touch,
        tile_count[0].astype(jnp.int32),
        slab_blocks,
        whole_table.reshape(span_blocks, tile_edge, factor_width),
        ratings[0],
        n_slots,
    )
    send_rows = send_rows.reshape(owners, CAP * tile_edge, factor_width)
    arrived, arrived_ids = (
        lax.all_to_all(send_rows, "item", split_axis=0, concat_axis=0, tiled=True),
        lax.all_to_all(request, "item", split_axis=0, concat_axis=0, tiled=True),
    )
    factors_new, mean_new, square_new = owner_update(
        arrived_ids.reshape(-1).astype(jnp.int32),
        arrived.reshape(owners * CAP, tile_edge, factor_width),
        item_factors,
        item_mean,
        item_square,
    )
    user_gradient = lax.psum_scatter(
        user_total.reshape(-1, factor_width),
        "band",
        scatter_dimension=0,
        tiled=True,
    )
    return (user_gradient, factors_new, mean_new, square_new)


def solution(mesh):
    in_specs = (
        P(("band", "item"), None),
        P(("band", "item"), None),
        P(("band", "item"), None),
        P(("band", "item"), None),
        P("band", "item", None, None),
        P("band", "item"),
        P("band", "item"),
        P("band", "item"),
    )
    out_specs = (
        P(("band", "item"), None),
        P(("band", "item"), None),
        P(("band", "item"), None),
        P(("band", "item"), None),
    )
    return jax.shard_map(body, mesh=mesh, in_specs=in_specs, out_specs=out_specs, check_vma=False)
```

```python
import jax
import jax.numpy as jnp
from jax import lax
from jax.sharding import PartitionSpec as P
from jax.experimental import pallas as pl
from jax.experimental.pallas import tpu as pltpu

CAP = 2


huber_edge = 1.0
beta_first = 0.9
beta_second = 0.999
learn_rate = 0.05
adam_steps = 10.0
adam_epsilon = 1e-08


def adam_update(factors, moment_old, square_old, gradient):
    moment_new = beta_first * moment_old + (1.0 - beta_first) * gradient
    square_new = beta_second * square_old + (1.0 - beta_second) * gradient * gradient
    moment_hat = moment_new / (1.0 - beta_first**adam_steps)
    square_hat = square_new / (1.0 - beta_second**adam_steps)
    factors_new = factors - learn_rate * moment_hat / (jnp.sqrt(square_hat) + adam_epsilon)
    return (factors_new, moment_new, square_new)


def _tile_kernel(users_ref, items_ref, slots_ref, first_ref, count_ref, slab_ref, table_ref, ratings_ref, user_out, send_out, acc_ref):
    user_out[...] = jnp.zeros(user_out.shape, user_out.dtype)
    count = count_ref[0]

    def step(t, carry):
        u = users_ref[t]
        j = items_ref[t]
        s = slots_ref[t]
        user_tile = slab_ref[u]
        item_tile = table_ref[j]
        residual = lax.dot_general(user_tile, item_tile, (((1,), (1,)), ((), ())), preferred_element_type=jnp.float32)
        residual = residual - ratings_ref[t].astype(jnp.float32)
        slope = jnp.where(t < count, jnp.clip(residual, -1.0, 1.0), 0.0)
        user_out[u] += jnp.dot(slope.astype(jnp.bfloat16), item_tile, preferred_element_type=jnp.float32)
        fresh = jnp.dot(slope.T.astype(jnp.bfloat16), user_tile, preferred_element_type=jnp.float32)
        acc_ref[s] = jnp.where(first_ref[t] > 0, fresh, acc_ref[s] + fresh)
        return carry

    lax.fori_loop(0, ratings_ref.shape[0], step, 0, unroll=8)
    send_out[...] = acc_ref[...].astype(send_out.dtype)


def tile_work(users, items, slots, first, count, slab, table, ratings, n_slots, interpret=False):
    vmem = pltpu.MemorySpace.VMEM if hasattr(pltpu, "MemorySpace") else pltpu.VMEM
    edge, width = slab.shape[1], slab.shape[2]
    return pl.pallas_call(
        _tile_kernel,
        grid_spec=pltpu.PrefetchScalarGridSpec(
            num_scalar_prefetch=5,
            grid=(1,),
            in_specs=[pl.BlockSpec(memory_space=vmem)] * 3,
            out_specs=[pl.BlockSpec(memory_space=vmem)] * 2,
            scratch_shapes=[pltpu.VMEM((n_slots, edge, width), jnp.float32)],
        ),
        out_shape=[
            jax.ShapeDtypeStruct(slab.shape, jnp.float32),
            jax.ShapeDtypeStruct((n_slots, edge, width), jnp.bfloat16),
        ],
        compiler_params=pltpu.CompilerParams(vmem_limit_bytes=56 * 1024 * 1024),
        interpret=interpret,
    )(users, items, slots, first, count, slab, table, ratings)


def _owner_kernel(ids_ref, arrived_ref, factors_ref, mean_ref, square_ref, factors_out, mean_out, square_out, acc_ref):
    acc_ref[...] = jnp.zeros(acc_ref.shape, acc_ref.dtype)
    edge = arrived_ref.shape[1]
    owned = acc_ref.shape[0] // edge

    def step(r, carry):
        block = ids_ref[r]
        rows = arrived_ref[r].astype(jnp.float32)
        start = pl.multiple_of(jnp.clip(block, 0, owned - 1) * edge, edge)
        acc_ref[pl.ds(start, edge), :] += jnp.where(block >= 0, rows, 0.0)
        return carry

    lax.fori_loop(0, arrived_ref.shape[0], step, 0, unroll=4)
    factors_new, mean_new, square_new = adam_update(factors_ref[...], mean_ref[...], square_ref[...], acc_ref[...])
    factors_out[...] = factors_new
    mean_out[...] = mean_new
    square_out[...] = square_new


def owner_update(ids, arrived, factors, mean, square, interpret=False):
    vmem = pltpu.MemorySpace.VMEM if hasattr(pltpu, "MemorySpace") else pltpu.VMEM
    out = jax.ShapeDtypeStruct(factors.shape, jnp.float32)
    return pl.pallas_call(
        _owner_kernel,
        grid_spec=pltpu.PrefetchScalarGridSpec(
            num_scalar_prefetch=1,
            grid=(1,),
            in_specs=[pl.BlockSpec(memory_space=vmem)] * 4,
            out_specs=[pl.BlockSpec(memory_space=vmem)] * 3,
            scratch_shapes=[pltpu.VMEM(factors.shape, jnp.float32)],
        ),
        out_shape=[out, out, out],
        compiler_params=pltpu.CompilerParams(vmem_limit_bytes=48 * 1024 * 1024),
        interpret=interpret,
    )(ids, arrived, factors, mean, square)


def body(
    user_factors, item_factors, item_mean, item_square, ratings, tile_users, tile_items, tile_count
):
    factor_width = user_factors.shape[1]
    tile_edge = ratings.shape[2]
    tile_slots = ratings.shape[1]
    owned_blocks = item_factors.shape[0] // tile_edge
    owners = lax.axis_size("item")
    span_blocks = owned_blocks * owners
    users_here = tile_users[0]
    items_here = tile_items[0]
    is_valid = jnp.arange(tile_slots, dtype=jnp.int32) < tile_count[0, 0]
    bands = lax.axis_size("band")
    slab_blocks = lax.all_to_all(
        jnp.broadcast_to(user_factors[None], (bands,) + user_factors.shape),
        "band", split_axis=0, concat_axis=0, tiled=True,
    ).reshape(-1, tile_edge, factor_width)
    block_hits = (
        items_here[None, :] == jnp.arange(span_blocks, dtype=jnp.int32)[:, None]
    ) & is_valid[None, :]
    touched = jnp.any(block_hits, axis=1).reshape(owners, owned_blocks).astype(jnp.int32)
    slot_rank = jnp.cumsum(touched, axis=1) - touched
    slot_match = (slot_rank[:, :, None] == jnp.arange(CAP, dtype=jnp.int32)[None, None, :]) & (
        touched[:, :, None] == 1
    )
    local_ids = jnp.arange(owned_blocks, dtype=jnp.int32)[None, :, None] + 1
    request = jnp.sum(jnp.where(slot_match, local_ids, 0), axis=1) - 1
    tile_slot = items_here // owned_blocks * CAP + slot_rank.reshape(-1)[items_here]
    whole_table = lax.all_gather(item_factors.astype(jnp.bfloat16), "item", axis=0, tiled=True)
    n_slots = owners * CAP
    tile_slot = jnp.clip(tile_slot, 0, n_slots - 1).astype(jnp.int32)
    slot_order = jnp.arange(tile_slots, dtype=jnp.int32)
    seen_before = (tile_slot[None, :] == tile_slot[:, None]) & (slot_order[None, :] < slot_order[:, None])
    first_touch = jnp.logical_not(jnp.any(seen_before, axis=1)).astype(jnp.int32)
    user_total, send_rows = tile_work(
        jnp.clip(users_here, 0, slab_blocks.shape[0] - 1).astype(jnp.int32),
        jnp.clip(items_here, 0, span_blocks - 1).astype(jnp.int32),
        tile_slot,
        first_touch,
        tile_count[0].astype(jnp.int32),
        slab_blocks,
        whole_table.reshape(span_blocks, tile_edge, factor_width),
        ratings[0],
        n_slots,
    )
    send_rows = send_rows.reshape(owners, CAP * tile_edge, factor_width)
    arrived, arrived_ids = (
        lax.all_to_all(send_rows, "item", split_axis=0, concat_axis=0, tiled=True),
        lax.all_to_all(request, "item", split_axis=0, concat_axis=0, tiled=True),
    )
    factors_new, mean_new, square_new = owner_update(
        arrived_ids.reshape(-1).astype(jnp.int32),
        arrived.reshape(owners * CAP, tile_edge, factor_width),
        item_factors,
        item_mean,
        item_square,
    )
    user_gradient = lax.psum_scatter(
        user_total.reshape(-1, factor_width),
        "band",
        scatter_dimension=0,
        tiled=True,
    )
    return (user_gradient, factors_new, mean_new, square_new)


def solution(mesh):
    in_specs = (
        P(("band", "item"), None),
        P(("band", "item"), None),
        P(("band", "item"), None),
        P(("band", "item"), None),
        P("band", "item", None, None),
        P("band", "item"),
        P("band", "item"),
        P("band", "item"),
    )
    out_specs = (
        P(("band", "item"), None),
        P(("band", "item"), None),
        P(("band", "item"), None),
        P(("band", "item"), None),
    )
    return jax.shard_map(body, mesh=mesh, in_specs=in_specs, out_specs=out_specs, check_vma=False)
```

```python
import jax
import jax.numpy as jnp
from jax import lax
from jax.sharding import PartitionSpec as P
from jax.experimental import pallas as pl
from jax.experimental.pallas import tpu as pltpu

CAP = 2


huber_edge = 1.0
beta_first = 0.9
beta_second = 0.999
learn_rate = 0.05
adam_steps = 10.0
adam_epsilon = 1e-08


def adam_update(factors, moment_old, square_old, gradient):
    moment_new = beta_first * moment_old + (1.0 - beta_first) * gradient
    square_new = beta_second * square_old + (1.0 - beta_second) * gradient * gradient
    moment_hat = moment_new / (1.0 - beta_first**adam_steps)
    square_hat = square_new / (1.0 - beta_second**adam_steps)
    factors_new = factors - learn_rate * moment_hat / (jnp.sqrt(square_hat) + adam_epsilon)
    return (factors_new, moment_new, square_new)


def _tile_kernel(users_ref, items_ref, slots_ref, first_ref, count_ref, slab_ref, table_ref, ratings_ref, user_out, send_out, acc_ref):
    user_out[...] = jnp.zeros(user_out.shape, user_out.dtype)
    count = count_ref[0]

    def step(t, carry):
        u = users_ref[t]
        j = items_ref[t]
        s = slots_ref[t]
        user_tile = slab_ref[u]
        item_tile = table_ref[j]
        residual = lax.dot_general(user_tile, item_tile, (((1,), (1,)), ((), ())), preferred_element_type=jnp.float32)
        residual = residual - ratings_ref[t].astype(jnp.float32)
        slope = jnp.where(t < count, jnp.clip(residual, -1.0, 1.0), 0.0)
        slope_bf16 = slope.astype(jnp.bfloat16)
        user_out[u] += jnp.dot(slope_bf16, item_tile, preferred_element_type=jnp.float32)
        fresh = lax.dot_general(slope_bf16, user_tile, (((0,), (0,)), ((), ())), preferred_element_type=jnp.float32)
        acc_ref[s] = jnp.where(first_ref[t] > 0, fresh, acc_ref[s] + fresh)
        return carry

    lax.fori_loop(0, ratings_ref.shape[0], step, 0, unroll=8)
    send_out[...] = acc_ref[...].astype(send_out.dtype)


def tile_work(users, items, slots, first, count, slab, table, ratings, n_slots, interpret=False):
    vmem = pltpu.MemorySpace.VMEM if hasattr(pltpu, "MemorySpace") else pltpu.VMEM
    edge, width = slab.shape[1], slab.shape[2]
    return pl.pallas_call(
        _tile_kernel,
        grid_spec=pltpu.PrefetchScalarGridSpec(
            num_scalar_prefetch=5,
            grid=(1,),
            in_specs=[pl.BlockSpec(memory_space=vmem)] * 3,
            out_specs=[pl.BlockSpec(memory_space=vmem)] * 2,
            scratch_shapes=[pltpu.VMEM((n_slots, edge, width), jnp.float32)],
        ),
        out_shape=[
            jax.ShapeDtypeStruct(slab.shape, jnp.float32),
            jax.ShapeDtypeStruct((n_slots, edge, width), jnp.bfloat16),
        ],
        compiler_params=pltpu.CompilerParams(vmem_limit_bytes=56 * 1024 * 1024),
        interpret=interpret,
    )(users, items, slots, first, count, slab, table, ratings)


def _owner_kernel(ids_ref, arrived_ref, factors_ref, mean_ref, square_ref, factors_out, mean_out, square_out, acc_ref):
    acc_ref[...] = jnp.zeros(acc_ref.shape, acc_ref.dtype)
    edge = arrived_ref.shape[1]
    owned = acc_ref.shape[0] // edge

    def step(r, carry):
        block = ids_ref[r]
        rows = arrived_ref[r].astype(jnp.float32)
        start = pl.multiple_of(jnp.clip(block, 0, owned - 1) * edge, edge)
        acc_ref[pl.ds(start, edge), :] += jnp.where(block >= 0, rows, 0.0)
        return carry

    lax.fori_loop(0, arrived_ref.shape[0], step, 0, unroll=4)
    factors_new, mean_new, square_new = adam_update(factors_ref[...], mean_ref[...], square_ref[...], acc_ref[...])
    factors_out[...] = factors_new
    mean_out[...] = mean_new
    square_out[...] = square_new


def owner_update(ids, arrived, factors, mean, square, interpret=False):
    vmem = pltpu.MemorySpace.VMEM if hasattr(pltpu, "MemorySpace") else pltpu.VMEM
    out = jax.ShapeDtypeStruct(factors.shape, jnp.float32)
    return pl.pallas_call(
        _owner_kernel,
        grid_spec=pltpu.PrefetchScalarGridSpec(
            num_scalar_prefetch=1,
            grid=(1,),
            in_specs=[pl.BlockSpec(memory_space=vmem)] * 4,
            out_specs=[pl.BlockSpec(memory_space=vmem)] * 3,
            scratch_shapes=[pltpu.VMEM(factors.shape, jnp.float32)],
        ),
        out_shape=[out, out, out],
        compiler_params=pltpu.CompilerParams(vmem_limit_bytes=48 * 1024 * 1024),
        interpret=interpret,
    )(ids, arrived, factors, mean, square)


def body(
    user_factors, item_factors, item_mean, item_square, ratings, tile_users, tile_items, tile_count
):
    factor_width = user_factors.shape[1]
    tile_edge = ratings.shape[2]
    tile_slots = ratings.shape[1]
    owned_blocks = item_factors.shape[0] // tile_edge
    owners = lax.axis_size("item")
    span_blocks = owned_blocks * owners
    users_here = tile_users[0]
    items_here = tile_items[0]
    is_valid = jnp.arange(tile_slots, dtype=jnp.int32) < tile_count[0, 0]
    bands = lax.axis_size("band")
    slab_blocks = lax.all_to_all(
        jnp.broadcast_to(user_factors[None], (bands,) + user_factors.shape),
        "band", split_axis=0, concat_axis=0, tiled=True,
    ).reshape(-1, tile_edge, factor_width)
    block_hits = (
        items_here[None, :] == jnp.arange(span_blocks, dtype=jnp.int32)[:, None]
    ) & is_valid[None, :]
    touched = jnp.any(block_hits, axis=1).reshape(owners, owned_blocks).astype(jnp.int32)
    slot_rank = jnp.cumsum(touched, axis=1) - touched
    slot_match = (slot_rank[:, :, None] == jnp.arange(CAP, dtype=jnp.int32)[None, None, :]) & (
        touched[:, :, None] == 1
    )
    local_ids = jnp.arange(owned_blocks, dtype=jnp.int32)[None, :, None] + 1
    request = jnp.sum(jnp.where(slot_match, local_ids, 0), axis=1) - 1
    tile_slot = items_here // owned_blocks * CAP + slot_rank.reshape(-1)[items_here]
    whole_table = lax.all_gather(item_factors.astype(jnp.bfloat16), "item", axis=0, tiled=True)
    n_slots = owners * CAP
    tile_slot = jnp.clip(tile_slot, 0, n_slots - 1).astype(jnp.int32)
    slot_order = jnp.arange(tile_slots, dtype=jnp.int32)
    seen_before = (tile_slot[None, :] == tile_slot[:, None]) & (slot_order[None, :] < slot_order[:, None])
    first_touch = jnp.logical_not(jnp.any(seen_before, axis=1)).astype(jnp.int32)
    user_total, send_rows = tile_work(
        jnp.clip(users_here, 0, slab_blocks.shape[0] - 1).astype(jnp.int32),
        jnp.clip(items_here, 0, span_blocks - 1).astype(jnp.int32),
        tile_slot,
        first_touch,
        tile_count[0].astype(jnp.int32),
        slab_blocks,
        whole_table.reshape(span_blocks, tile_edge, factor_width),
        ratings[0],
        n_slots,
    )
    send_rows = send_rows.reshape(owners, CAP * tile_edge, factor_width)
    arrived, arrived_ids = (
        lax.all_to_all(send_rows, "item", split_axis=0, concat_axis=0, tiled=True),
        lax.all_to_all(request, "item", split_axis=0, concat_axis=0, tiled=True),
    )
    factors_new, mean_new, square_new = owner_update(
        arrived_ids.reshape(-1).astype(jnp.int32),
        arrived.reshape(owners * CAP, tile_edge, factor_width),
        item_factors,
        item_mean,
        item_square,
    )
    user_gradient = lax.psum_scatter(
        user_total.reshape(-1, factor_width),
        "band",
        scatter_dimension=0,
        tiled=True,
    )
    return (user_gradient, factors_new, mean_new, square_new)


def solution(mesh):
    in_specs = (
        P(("band", "item"), None),
        P(("band", "item"), None),
        P(("band", "item"), None),
        P(("band", "item"), None),
        P("band", "item", None, None),
        P("band", "item"),
        P("band", "item"),
        P("band", "item"),
    )
    out_specs = (
        P(("band", "item"), None),
        P(("band", "item"), None),
        P(("band", "item"), None),
        P(("band", "item"), None),
    )
    return jax.shard_map(body, mesh=mesh, in_specs=in_specs, out_specs=out_specs, check_vma=False)
```

```python
import jax
import jax.numpy as jnp
from jax import lax
from jax.sharding import PartitionSpec as P
from jax.experimental import pallas as pl
from jax.experimental.pallas import tpu as pltpu

CAP = 2


huber_edge = 1.0
beta_first = 0.9
beta_second = 0.999
learn_rate = 0.05
adam_steps = 10.0
adam_epsilon = 1e-08


def adam_update(factors, moment_old, square_old, gradient):
    moment_new = beta_first * moment_old + (1.0 - beta_first) * gradient
    square_new = beta_second * square_old + (1.0 - beta_second) * gradient * gradient
    moment_hat = moment_new / (1.0 - beta_first**adam_steps)
    square_hat = square_new / (1.0 - beta_second**adam_steps)
    factors_new = factors - learn_rate * moment_hat / (jnp.sqrt(square_hat) + adam_epsilon)
    return (factors_new, moment_new, square_new)


def _tile_kernel(users_ref, items_ref, slots_ref, first_ref, count_ref, slab_ref, table_ref, ratings_ref, user_out, send_out, acc_ref):
    user_out[...] = jnp.zeros(user_out.shape, user_out.dtype)
    count = count_ref[0]

    def step(t, carry):
        u = users_ref[t]
        j = items_ref[t]
        s = slots_ref[t]
        user_tile = slab_ref[u]
        item_tile = table_ref[j]
        residual = lax.dot_general(user_tile, item_tile, (((1,), (1,)), ((), ())), preferred_element_type=jnp.float32)
        residual = residual - ratings_ref[t].astype(jnp.float32)
        slope = jnp.where(t < count, jnp.clip(residual, -1.0, 1.0), 0.0)
        user_out[u] += jnp.dot(slope.astype(jnp.bfloat16), item_tile, preferred_element_type=jnp.float32)
        fresh = jnp.dot(slope.T.astype(jnp.bfloat16), user_tile, preferred_element_type=jnp.float32)
        acc_ref[s] = jnp.where(first_ref[t] > 0, fresh, acc_ref[s] + fresh)
        return carry

    lax.fori_loop(0, ratings_ref.shape[0], step, 0, unroll=13)
    send_out[...] = acc_ref[...].astype(send_out.dtype)


def tile_work(users, items, slots, first, count, slab, table, ratings, n_slots, interpret=False):
    vmem = pltpu.MemorySpace.VMEM if hasattr(pltpu, "MemorySpace") else pltpu.VMEM
    edge, width = slab.shape[1], slab.shape[2]
    return pl.pallas_call(
        _tile_kernel,
        grid_spec=pltpu.PrefetchScalarGridSpec(
            num_scalar_prefetch=5,
            grid=(1,),
            in_specs=[pl.BlockSpec(memory_space=vmem)] * 3,
            out_specs=[pl.BlockSpec(memory_space=vmem)] * 2,
            scratch_shapes=[pltpu.VMEM((n_slots, edge, width), jnp.float32)],
        ),
        out_shape=[
            jax.ShapeDtypeStruct(slab.shape, jnp.float32),
            jax.ShapeDtypeStruct((n_slots, edge, width), jnp.bfloat16),
        ],
        compiler_params=pltpu.CompilerParams(vmem_limit_bytes=56 * 1024 * 1024),
        interpret=interpret,
    )(users, items, slots, first, count, slab, table, ratings)


def _owner_kernel(ids_ref, arrived_ref, factors_ref, mean_ref, square_ref, factors_out, mean_out, square_out, acc_ref):
    acc_ref[...] = jnp.zeros(acc_ref.shape, acc_ref.dtype)
    edge = arrived_ref.shape[1]
    owned = acc_ref.shape[0] // edge

    def step(r, carry):
        block = ids_ref[r]
        rows = arrived_ref[r].astype(jnp.float32)
        start = pl.multiple_of(jnp.clip(block, 0, owned - 1) * edge, edge)
        acc_ref[pl.ds(start, edge), :] += jnp.where(block >= 0, rows, 0.0)
        return carry

    lax.fori_loop(0, arrived_ref.shape[0], step, 0, unroll=8)
    factors_new, mean_new, square_new = adam_update(factors_ref[...], mean_ref[...], square_ref[...], acc_ref[...])
    factors_out[...] = factors_new
    mean_out[...] = mean_new
    square_out[...] = square_new


def owner_update(ids, arrived, factors, mean, square, interpret=False):
    vmem = pltpu.MemorySpace.VMEM if hasattr(pltpu, "MemorySpace") else pltpu.VMEM
    out = jax.ShapeDtypeStruct(factors.shape, jnp.float32)
    return pl.pallas_call(
        _owner_kernel,
        grid_spec=pltpu.PrefetchScalarGridSpec(
            num_scalar_prefetch=1,
            grid=(1,),
            in_specs=[pl.BlockSpec(memory_space=vmem)] * 4,
            out_specs=[pl.BlockSpec(memory_space=vmem)] * 3,
            scratch_shapes=[pltpu.VMEM(factors.shape, jnp.float32)],
        ),
        out_shape=[out, out, out],
        compiler_params=pltpu.CompilerParams(vmem_limit_bytes=48 * 1024 * 1024),
        interpret=interpret,
    )(ids, arrived, factors, mean, square)


def body(
    user_factors, item_factors, item_mean, item_square, ratings, tile_users, tile_items, tile_count
):
    factor_width = user_factors.shape[1]
    tile_edge = ratings.shape[2]
    tile_slots = ratings.shape[1]
    owned_blocks = item_factors.shape[0] // tile_edge
    owners = lax.axis_size("item")
    span_blocks = owned_blocks * owners
    users_here = tile_users[0]
    items_here = tile_items[0]
    is_valid = jnp.arange(tile_slots, dtype=jnp.int32) < tile_count[0, 0]
    bands = lax.axis_size("band")
    slab_blocks = lax.all_to_all(
        jnp.broadcast_to(user_factors[None], (bands,) + user_factors.shape),
        "band", split_axis=0, concat_axis=0, tiled=True,
    ).reshape(-1, tile_edge, factor_width)
    block_hits = (
        items_here[None, :] == jnp.arange(span_blocks, dtype=jnp.int32)[:, None]
    ) & is_valid[None, :]
    touched = jnp.any(block_hits, axis=1).reshape(owners, owned_blocks).astype(jnp.int32)
    slot_rank = jnp.cumsum(touched, axis=1) - touched
    slot_match = (slot_rank[:, :, None] == jnp.arange(CAP, dtype=jnp.int32)[None, None, :]) & (
        touched[:, :, None] == 1
    )
    local_ids = jnp.arange(owned_blocks, dtype=jnp.int32)[None, :, None] + 1
    request = jnp.sum(jnp.where(slot_match, local_ids, 0), axis=1) - 1
    tile_slot = items_here // owned_blocks * CAP + slot_rank.reshape(-1)[items_here]
    whole_table = lax.all_gather(item_factors.astype(jnp.bfloat16), "item", axis=0, tiled=True)
    n_slots = owners * CAP
    tile_slot = jnp.clip(tile_slot, 0, n_slots - 1).astype(jnp.int32)
    slot_order = jnp.arange(tile_slots, dtype=jnp.int32)
    seen_before = (tile_slot[None, :] == tile_slot[:, None]) & (slot_order[None, :] < slot_order[:, None])
    first_touch = jnp.logical_not(jnp.any(seen_before, axis=1)).astype(jnp.int32)
    user_total, send_rows = tile_work(
        jnp.clip(users_here, 0, slab_blocks.shape[0] - 1).astype(jnp.int32),
        jnp.clip(items_here, 0, span_blocks - 1).astype(jnp.int32),
        tile_slot,
        first_touch,
        tile_count[0].astype(jnp.int32),
        slab_blocks,
        whole_table.reshape(span_blocks, tile_edge, factor_width),
        ratings[0],
        n_slots,
    )
    send_rows = send_rows.reshape(owners, CAP * tile_edge, factor_width)
    arrived, arrived_ids = (
        lax.all_to_all(send_rows, "item", split_axis=0, concat_axis=0, tiled=True),
        lax.all_to_all(request, "item", split_axis=0, concat_axis=0, tiled=True),
    )
    factors_new, mean_new, square_new = owner_update(
        arrived_ids.reshape(-1).astype(jnp.int32),
        arrived.reshape(owners * CAP, tile_edge, factor_width),
        item_factors,
        item_mean,
        item_square,
    )
    user_gradient = lax.psum_scatter(
        user_total.reshape(-1, factor_width),
        "band",
        scatter_dimension=0,
        tiled=True,
    )
    return (user_gradient, factors_new, mean_new, square_new)


def solution(mesh):
    in_specs = (
        P(("band", "item"), None),
        P(("band", "item"), None),
        P(("band", "item"), None),
        P(("band", "item"), None),
        P("band", "item", None, None),
        P("band", "item"),
        P("band", "item"),
        P("band", "item"),
    )
    out_specs = (
        P(("band", "item"), None),
        P(("band", "item"), None),
        P(("band", "item"), None),
        P(("band", "item"), None),
    )
    return jax.shard_map(body, mesh=mesh, in_specs=in_specs, out_specs=out_specs, check_vma=False)
```

```python
import jax
import jax.numpy as jnp
from jax import lax
from jax.sharding import PartitionSpec as P
from jax.experimental import pallas as pl
from jax.experimental.pallas import tpu as pltpu

CAP = 2


huber_edge = 1.0
beta_first = 0.9
beta_second = 0.999
learn_rate = 0.05
adam_steps = 10.0
adam_epsilon = 1e-08


def adam_update(factors, moment_old, square_old, gradient):
    moment_new = beta_first * moment_old + (1.0 - beta_first) * gradient
    square_new = beta_second * square_old + (1.0 - beta_second) * gradient * gradient
    moment_hat = moment_new / (1.0 - beta_first**adam_steps)
    square_hat = square_new / (1.0 - beta_second**adam_steps)
    factors_new = factors - learn_rate * moment_hat / (jnp.sqrt(square_hat) + adam_epsilon)
    return (factors_new, moment_new, square_new)


def _tile_kernel(users_ref, items_ref, slots_ref, first_ref, count_ref, slab_ref, table_ref, ratings_ref, user_out, send_out, acc_ref):
    user_out[...] = jnp.zeros(user_out.shape, user_out.dtype)
    count = count_ref[0]

    def step(t, carry):
        u = users_ref[t]
        j = items_ref[t]
        s = slots_ref[t]
        user_tile = slab_ref[u]
        item_tile = table_ref[j]
        residual = lax.dot_general(user_tile, item_tile, (((1,), (1,)), ((), ())), preferred_element_type=jnp.float32)
        residual = residual - ratings_ref[t].astype(jnp.float32)
        slope = jnp.where(t < count, jnp.clip(residual, -1.0, 1.0), 0.0)
        user_out[u] += jnp.dot(slope.astype(jnp.bfloat16), item_tile, preferred_element_type=jnp.float32)
        fresh = jnp.dot(slope.T.astype(jnp.bfloat16), user_tile, preferred_element_type=jnp.float32)
        acc_ref[s] = jnp.where(first_ref[t] > 0, fresh, acc_ref[s] + fresh)
        return carry

    lax.fori_loop(0, ratings_ref.shape[0], step, 0, unroll=True)
    send_out[...] = acc_ref[...].astype(send_out.dtype)


def tile_work(users, items, slots, first, count, slab, table, ratings, n_slots, interpret=False):
    vmem = pltpu.MemorySpace.VMEM if hasattr(pltpu, "MemorySpace") else pltpu.VMEM
    edge, width = slab.shape[1], slab.shape[2]
    return pl.pallas_call(
        _tile_kernel,
        grid_spec=pltpu.PrefetchScalarGridSpec(
            num_scalar_prefetch=5,
            grid=(1,),
            in_specs=[pl.BlockSpec(memory_space=vmem)] * 3,
            out_specs=[pl.BlockSpec(memory_space=vmem)] * 2,
            scratch_shapes=[pltpu.VMEM((n_slots, edge, width), jnp.float32)],
        ),
        out_shape=[
            jax.ShapeDtypeStruct(slab.shape, jnp.float32),
            jax.ShapeDtypeStruct((n_slots, edge, width), jnp.bfloat16),
        ],
        compiler_params=pltpu.CompilerParams(vmem_limit_bytes=56 * 1024 * 1024),
        interpret=interpret,
    )(users, items, slots, first, count, slab, table, ratings)


def _owner_kernel(ids_ref, arrived_ref, factors_ref, mean_ref, square_ref, factors_out, mean_out, square_out, acc_ref):
    acc_ref[...] = jnp.zeros(acc_ref.shape, acc_ref.dtype)
    edge = arrived_ref.shape[1]
    owned = acc_ref.shape[0] // edge

    def step(r, carry):
        block = ids_ref[r]
        rows = arrived_ref[r].astype(jnp.float32)
        start = pl.multiple_of(jnp.clip(block, 0, owned - 1) * edge, edge)
        acc_ref[pl.ds(start, edge), :] += jnp.where(block >= 0, rows, 0.0)
        return carry

    lax.fori_loop(0, arrived_ref.shape[0], step, 0, unroll=8)
    factors_new, mean_new, square_new = adam_update(factors_ref[...], mean_ref[...], square_ref[...], acc_ref[...])
    factors_out[...] = factors_new
    mean_out[...] = mean_new
    square_out[...] = square_new


def owner_update(ids, arrived, factors, mean, square, interpret=False):
    vmem = pltpu.MemorySpace.VMEM if hasattr(pltpu, "MemorySpace") else pltpu.VMEM
    out = jax.ShapeDtypeStruct(factors.shape, jnp.float32)
    return pl.pallas_call(
        _owner_kernel,
        grid_spec=pltpu.PrefetchScalarGridSpec(
            num_scalar_prefetch=1,
            grid=(1,),
            in_specs=[pl.BlockSpec(memory_space=vmem)] * 4,
            out_specs=[pl.BlockSpec(memory_space=vmem)] * 3,
            scratch_shapes=[pltpu.VMEM(factors.shape, jnp.float32)],
        ),
        out_shape=[out, out, out],
        compiler_params=pltpu.CompilerParams(vmem_limit_bytes=48 * 1024 * 1024),
        interpret=interpret,
    )(ids, arrived, factors, mean, square)


def body(
    user_factors, item_factors, item_mean, item_square, ratings, tile_users, tile_items, tile_count
):
    factor_width = user_factors.shape[1]
    tile_edge = ratings.shape[2]
    tile_slots = ratings.shape[1]
    owned_blocks = item_factors.shape[0] // tile_edge
    owners = lax.axis_size("item")
    span_blocks = owned_blocks * owners
    users_here = tile_users[0]
    items_here = tile_items[0]
    is_valid = jnp.arange(tile_slots, dtype=jnp.int32) < tile_count[0, 0]
    bands = lax.axis_size("band")
    slab_blocks = lax.all_to_all(
        jnp.broadcast_to(user_factors[None], (bands,) + user_factors.shape),
        "band", split_axis=0, concat_axis=0, tiled=True,
    ).reshape(-1, tile_edge, factor_width)
    block_hits = (
        items_here[None, :] == jnp.arange(span_blocks, dtype=jnp.int32)[:, None]
    ) & is_valid[None, :]
    touched = jnp.any(block_hits, axis=1).reshape(owners, owned_blocks).astype(jnp.int32)
    slot_rank = jnp.cumsum(touched, axis=1) - touched
    slot_match = (slot_rank[:, :, None] == jnp.arange(CAP, dtype=jnp.int32)[None, None, :]) & (
        touched[:, :, None] == 1
    )
    local_ids = jnp.arange(owned_blocks, dtype=jnp.int32)[None, :, None] + 1
    request = jnp.sum(jnp.where(slot_match, local_ids, 0), axis=1) - 1
    tile_slot = items_here // owned_blocks * CAP + slot_rank.reshape(-1)[items_here]
    whole_table = lax.all_gather(item_factors.astype(jnp.bfloat16), "item", axis=0, tiled=True)
    n_slots = owners * CAP
    tile_slot = jnp.clip(tile_slot, 0, n_slots - 1).astype(jnp.int32)
    slot_order = jnp.arange(tile_slots, dtype=jnp.int32)
    seen_before = (tile_slot[None, :] == tile_slot[:, None]) & (slot_order[None, :] < slot_order[:, None])
    first_touch = jnp.logical_not(jnp.any(seen_before, axis=1)).astype(jnp.int32)
    user_total, send_rows = tile_work(
        jnp.clip(users_here, 0, slab_blocks.shape[0] - 1).astype(jnp.int32),
        jnp.clip(items_here, 0, span_blocks - 1).astype(jnp.int32),
        tile_slot,
        first_touch,
        tile_count[0].astype(jnp.int32),
        slab_blocks,
        whole_table.reshape(span_blocks, tile_edge, factor_width),
        ratings[0],
        n_slots,
    )
    send_rows = send_rows.reshape(owners, CAP * tile_edge, factor_width)
    arrived, arrived_ids = (
        lax.all_to_all(send_rows, "item", split_axis=0, concat_axis=0, tiled=True),
        lax.all_to_all(request, "item", split_axis=0, concat_axis=0, tiled=True),
    )
    factors_new, mean_new, square_new = owner_update(
        arrived_ids.reshape(-1).astype(jnp.int32),
        arrived.reshape(owners * CAP, tile_edge, factor_width),
        item_factors,
        item_mean,
        item_square,
    )
    user_gradient = lax.psum_scatter(
        user_total.reshape(-1, factor_width),
        "band",
        scatter_dimension=0,
        tiled=True,
    )
    return (user_gradient, factors_new, mean_new, square_new)


def solution(mesh):
    in_specs = (
        P(("band", "item"), None),
        P(("band", "item"), None),
        P(("band", "item"), None),
        P(("band", "item"), None),
        P("band", "item", None, None),
        P("band", "item"),
        P("band", "item"),
        P("band", "item"),
    )
    out_specs = (
        P(("band", "item"), None),
        P(("band", "item"), None),
        P(("band", "item"), None),
        P(("band", "item"), None),
    )
    return jax.shard_map(body, mesh=mesh, in_specs=in_specs, out_specs=out_specs, check_vma=False)
```

```python
import jax
import jax.numpy as jnp
from jax import lax
from jax.sharding import PartitionSpec as P
from jax.experimental import pallas as pl
from jax.experimental.pallas import tpu as pltpu

CAP = 2


huber_edge = 1.0
beta_first = 0.9
beta_second = 0.999
learn_rate = 0.05
adam_steps = 10.0
adam_epsilon = 1e-08


def adam_update(factors, moment_old, square_old, gradient):
    moment_new = beta_first * moment_old + (1.0 - beta_first) * gradient
    square_new = beta_second * square_old + (1.0 - beta_second) * gradient * gradient
    moment_hat = moment_new / (1.0 - beta_first**adam_steps)
    square_hat = square_new / (1.0 - beta_second**adam_steps)
    factors_new = factors - learn_rate * moment_hat / (jnp.sqrt(square_hat) + adam_epsilon)
    return (factors_new, moment_new, square_new)


def _tile_kernel(users_ref, items_ref, slots_ref, first_ref, count_ref, slab_ref, table_ref, ratings_ref, user_out, send_out, acc_ref):
    user_out[...] = jnp.zeros(user_out.shape, user_out.dtype)
    count = count_ref[0]

    def step(t, carry):
        u = users_ref[t]
        j = items_ref[t]
        s = slots_ref[t]
        user_tile = slab_ref[u]
        item_tile = table_ref[j]
        residual = lax.dot_general(user_tile, item_tile, (((1,), (1,)), ((), ())), preferred_element_type=jnp.float32)
        residual = residual - ratings_ref[t].astype(jnp.float32)
        slope = jnp.where(t < count, jnp.clip(residual, -1.0, 1.0), 0.0)
        user_out[u] += jnp.dot(slope.astype(jnp.bfloat16), item_tile, preferred_element_type=jnp.float32)
        fresh = jnp.dot(slope.T.astype(jnp.bfloat16), user_tile, preferred_element_type=jnp.float32)
        acc_ref[s] = jnp.where(first_ref[t] > 0, fresh, acc_ref[s] + fresh)
        return carry

    lax.fori_loop(0, ratings_ref.shape[0], step, 0, unroll=13)
    send_out[...] = acc_ref[...].astype(send_out.dtype)


def tile_work(users, items, slots, first, count, slab, table, ratings, n_slots, interpret=False):
    vmem = pltpu.MemorySpace.VMEM if hasattr(pltpu, "MemorySpace") else pltpu.VMEM
    edge, width = slab.shape[1], slab.shape[2]
    return pl.pallas_call(
        _tile_kernel,
        grid_spec=pltpu.PrefetchScalarGridSpec(
            num_scalar_prefetch=5,
            grid=(1,),
            in_specs=[pl.BlockSpec(memory_space=vmem)] * 3,
            out_specs=[pl.BlockSpec(memory_space=vmem)] * 2,
            scratch_shapes=[pltpu.VMEM((n_slots, edge, width), jnp.float32)],
        ),
        out_shape=[
            jax.ShapeDtypeStruct(slab.shape, jnp.float32),
            jax.ShapeDtypeStruct((n_slots, edge, width), jnp.bfloat16),
        ],
        compiler_params=pltpu.CompilerParams(vmem_limit_bytes=56 * 1024 * 1024),
        interpret=interpret,
    )(users, items, slots, first, count, slab, table, ratings)


def _owner_kernel(ids_ref, arrived_ref, factors_ref, mean_ref, square_ref, factors_out, mean_out, square_out, acc_ref):
    acc_ref[...] = jnp.zeros(acc_ref.shape, acc_ref.dtype)
    edge = arrived_ref.shape[1]
    owned = acc_ref.shape[0] // edge

    def step(r, carry):
        block = ids_ref[r]
        rows = arrived_ref[r].astype(jnp.float32)
        start = pl.multiple_of(jnp.clip(block, 0, owned - 1) * edge, edge)
        acc_ref[pl.ds(start, edge), :] += jnp.where(block >= 0, rows, 0.0)
        return carry

    lax.fori_loop(0, arrived_ref.shape[0], step, 0, unroll=True)
    factors_new, mean_new, square_new = adam_update(factors_ref[...], mean_ref[...], square_ref[...], acc_ref[...])
    factors_out[...] = factors_new
    mean_out[...] = mean_new
    square_out[...] = square_new


def owner_update(ids, arrived, factors, mean, square, interpret=False):
    vmem = pltpu.MemorySpace.VMEM if hasattr(pltpu, "MemorySpace") else pltpu.VMEM
    out = jax.ShapeDtypeStruct(factors.shape, jnp.float32)
    return pl.pallas_call(
        _owner_kernel,
        grid_spec=pltpu.PrefetchScalarGridSpec(
            num_scalar_prefetch=1,
            grid=(1,),
            in_specs=[pl.BlockSpec(memory_space=vmem)] * 4,
            out_specs=[pl.BlockSpec(memory_space=vmem)] * 3,
            scratch_shapes=[pltpu.VMEM(factors.shape, jnp.float32)],
        ),
        out_shape=[out, out, out],
        compiler_params=pltpu.CompilerParams(vmem_limit_bytes=48 * 1024 * 1024),
        interpret=interpret,
    )(ids, arrived, factors, mean, square)


def body(
    user_factors, item_factors, item_mean, item_square, ratings, tile_users, tile_items, tile_count
):
    factor_width = user_factors.shape[1]
    tile_edge = ratings.shape[2]
    tile_slots = ratings.shape[1]
    owned_blocks = item_factors.shape[0] // tile_edge
    owners = lax.axis_size("item")
    span_blocks = owned_blocks * owners
    users_here = tile_users[0]
    items_here = tile_items[0]
    is_valid = jnp.arange(tile_slots, dtype=jnp.int32) < tile_count[0, 0]
    bands = lax.axis_size("band")
    slab_blocks = lax.all_to_all(
        jnp.broadcast_to(user_factors[None], (bands,) + user_factors.shape),
        "band", split_axis=0, concat_axis=0, tiled=True,
    ).reshape(-1, tile_edge, factor_width)
    block_hits = (
        items_here[None, :] == jnp.arange(span_blocks, dtype=jnp.int32)[:, None]
    ) & is_valid[None, :]
    touched = jnp.any(block_hits, axis=1).reshape(owners, owned_blocks).astype(jnp.int32)
    slot_rank = jnp.cumsum(touched, axis=1) - touched
    slot_match = (slot_rank[:, :, None] == jnp.arange(CAP, dtype=jnp.int32)[None, None, :]) & (
        touched[:, :, None] == 1
    )
    local_ids = jnp.arange(owned_blocks, dtype=jnp.int32)[None, :, None] + 1
    request = jnp.sum(jnp.where(slot_match, local_ids, 0), axis=1) - 1
    tile_slot = items_here // owned_blocks * CAP + slot_rank.reshape(-1)[items_here]
    whole_table = lax.all_gather(item_factors.astype(jnp.bfloat16), "item", axis=0, tiled=True)
    n_slots = owners * CAP
    tile_slot = jnp.clip(tile_slot, 0, n_slots - 1).astype(jnp.int32)
    slot_order = jnp.arange(tile_slots, dtype=jnp.int32)
    seen_before = (tile_slot[None, :] == tile_slot[:, None]) & (slot_order[None, :] < slot_order[:, None])
    first_touch = jnp.logical_not(jnp.any(seen_before, axis=1)).astype(jnp.int32)
    user_total, send_rows = tile_work(
        jnp.clip(users_here, 0, slab_blocks.shape[0] - 1).astype(jnp.int32),
        jnp.clip(items_here, 0, span_blocks - 1).astype(jnp.int32),
        tile_slot,
        first_touch,
        tile_count[0].astype(jnp.int32),
        slab_blocks,
        whole_table.reshape(span_blocks, tile_edge, factor_width),
        ratings[0],
        n_slots,
    )
    send_rows = send_rows.reshape(owners, CAP * tile_edge, factor_width)
    arrived, arrived_ids = (
        lax.all_to_all(send_rows, "item", split_axis=0, concat_axis=0, tiled=True),
        lax.all_to_all(request, "item", split_axis=0, concat_axis=0, tiled=True),
    )
    factors_new, mean_new, square_new = owner_update(
        arrived_ids.reshape(-1).astype(jnp.int32),
        arrived.reshape(owners * CAP, tile_edge, factor_width),
        item_factors,
        item_mean,
        item_square,
    )
    user_gradient = lax.psum_scatter(
        user_total.reshape(-1, factor_width),
        "band",
        scatter_dimension=0,
        tiled=True,
    )
    return (user_gradient, factors_new, mean_new, square_new)


def solution(mesh):
    in_specs = (
        P(("band", "item"), None),
        P(("band", "item"), None),
        P(("band", "item"), None),
        P(("band", "item"), None),
        P("band", "item", None, None),
        P("band", "item"),
        P("band", "item"),
        P("band", "item"),
    )
    out_specs = (
        P(("band", "item"), None),
        P(("band", "item"), None),
        P(("band", "item"), None),
        P(("band", "item"), None),
    )
    return jax.shard_map(body, mesh=mesh, in_specs=in_specs, out_specs=out_specs, check_vma=False)
```

```python
import jax
import jax.numpy as jnp
from jax import lax
from jax.sharding import PartitionSpec as P
from jax.experimental import pallas as pl
from jax.experimental.pallas import tpu as pltpu

CAP = 2


huber_edge = 1.0
beta_first = 0.9
beta_second = 0.999
learn_rate = 0.05
adam_steps = 10.0
adam_epsilon = 1e-08


def adam_update(factors, moment_old, square_old, gradient):
    moment_new = beta_first * moment_old + (1.0 - beta_first) * gradient
    square_new = beta_second * square_old + (1.0 - beta_second) * gradient * gradient
    moment_hat = moment_new / (1.0 - beta_first**adam_steps)
    square_hat = square_new / (1.0 - beta_second**adam_steps)
    factors_new = factors - learn_rate * moment_hat / (jnp.sqrt(square_hat) + adam_epsilon)
    return (factors_new, moment_new, square_new)


def _tile_kernel(users_ref, items_ref, slots_ref, first_ref, count_ref, slab_ref, table_ref, ratings_ref, user_out, send_out, acc_ref):
    user_out[...] = jnp.zeros(user_out.shape, user_out.dtype)
    count = count_ref[0]

    def step(t, carry):
        u = users_ref[t]
        j = items_ref[t]
        s = slots_ref[t]
        user_tile = slab_ref[u]
        item_tile = table_ref[j]
        residual = lax.dot_general(user_tile, item_tile, (((1,), (1,)), ((), ())), preferred_element_type=jnp.float32)
        residual = residual - ratings_ref[t].astype(jnp.float32)
        slope = jnp.where(t < count, jnp.clip(residual, -1.0, 1.0), 0.0)
        user_out[u] += jnp.dot(slope.astype(jnp.bfloat16), item_tile, preferred_element_type=jnp.float32)
        fresh = jnp.dot(slope.T.astype(jnp.bfloat16), user_tile, preferred_element_type=jnp.float32)
        acc_ref[s] = jnp.where(first_ref[t] > 0, fresh, acc_ref[s] + fresh)
        return carry

    lax.fori_loop(0, ratings_ref.shape[0], step, 0, unroll=26)
    send_out[...] = acc_ref[...].astype(send_out.dtype)


def tile_work(users, items, slots, first, count, slab, table, ratings, n_slots, interpret=False):
    vmem = pltpu.MemorySpace.VMEM if hasattr(pltpu, "MemorySpace") else pltpu.VMEM
    edge, width = slab.shape[1], slab.shape[2]
    return pl.pallas_call(
        _tile_kernel,
        grid_spec=pltpu.PrefetchScalarGridSpec(
            num_scalar_prefetch=5,
            grid=(1,),
            in_specs=[pl.BlockSpec(memory_space=vmem)] * 3,
            out_specs=[pl.BlockSpec(memory_space=vmem)] * 2,
            scratch_shapes=[pltpu.VMEM((n_slots, edge, width), jnp.float32)],
        ),
        out_shape=[
            jax.ShapeDtypeStruct(slab.shape, jnp.float32),
            jax.ShapeDtypeStruct((n_slots, edge, width), jnp.bfloat16),
        ],
        compiler_params=pltpu.CompilerParams(vmem_limit_bytes=56 * 1024 * 1024),
        interpret=interpret,
    )(users, items, slots, first, count, slab, table, ratings)


def _owner_kernel(ids_ref, arrived_ref, factors_ref, mean_ref, square_ref, factors_out, mean_out, square_out, acc_ref):
    acc_ref[...] = jnp.zeros(acc_ref.shape, acc_ref.dtype)
    edge = arrived_ref.shape[1]
    owned = acc_ref.shape[0] // edge

    def step(r, carry):
        block = ids_ref[r]
        rows = arrived_ref[r].astype(jnp.float32)
        start = pl.multiple_of(jnp.clip(block, 0, owned - 1) * edge, edge)
        acc_ref[pl.ds(start, edge), :] += jnp.where(block >= 0, rows, 0.0)
        return carry

    lax.fori_loop(0, arrived_ref.shape[0], step, 0, unroll=8)
    factors_new, mean_new, square_new = adam_update(factors_ref[...], mean_ref[...], square_ref[...], acc_ref[...])
    factors_out[...] = factors_new
    mean_out[...] = mean_new
    square_out[...] = square_new


def owner_update(ids, arrived, factors, mean, square, interpret=False):
    vmem = pltpu.MemorySpace.VMEM if hasattr(pltpu, "MemorySpace") else pltpu.VMEM
    out = jax.ShapeDtypeStruct(factors.shape, jnp.float32)
    return pl.pallas_call(
        _owner_kernel,
        grid_spec=pltpu.PrefetchScalarGridSpec(
            num_scalar_prefetch=1,
            grid=(1,),
            in_specs=[pl.BlockSpec(memory_space=vmem)] * 4,
            out_specs=[pl.BlockSpec(memory_space=vmem)] * 3,
            scratch_shapes=[pltpu.VMEM(factors.shape, jnp.float32)],
        ),
        out_shape=[out, out, out],
        compiler_params=pltpu.CompilerParams(vmem_limit_bytes=48 * 1024 * 1024),
        interpret=interpret,
    )(ids, arrived, factors, mean, square)


def body(
    user_factors, item_factors, item_mean, item_square, ratings, tile_users, tile_items, tile_count
):
    factor_width = user_factors.shape[1]
    tile_edge = ratings.shape[2]
    tile_slots = ratings.shape[1]
    owned_blocks = item_factors.shape[0] // tile_edge
    owners = lax.axis_size("item")
    span_blocks = owned_blocks * owners
    users_here = tile_users[0]
    items_here = tile_items[0]
    is_valid = jnp.arange(tile_slots, dtype=jnp.int32) < tile_count[0, 0]
    bands = lax.axis_size("band")
    slab_blocks = lax.all_to_all(
        jnp.broadcast_to(user_factors[None], (bands,) + user_factors.shape),
        "band", split_axis=0, concat_axis=0, tiled=True,
    ).reshape(-1, tile_edge, factor_width)
    block_hits = (
        items_here[None, :] == jnp.arange(span_blocks, dtype=jnp.int32)[:, None]
    ) & is_valid[None, :]
    touched = jnp.any(block_hits, axis=1).reshape(owners, owned_blocks).astype(jnp.int32)
    slot_rank = jnp.cumsum(touched, axis=1) - touched
    slot_match = (slot_rank[:, :, None] == jnp.arange(CAP, dtype=jnp.int32)[None, None, :]) & (
        touched[:, :, None] == 1
    )
    local_ids = jnp.arange(owned_blocks, dtype=jnp.int32)[None, :, None] + 1
    request = jnp.sum(jnp.where(slot_match, local_ids, 0), axis=1) - 1
    tile_slot = items_here // owned_blocks * CAP + slot_rank.reshape(-1)[items_here]
    whole_table = lax.all_gather(item_factors.astype(jnp.bfloat16), "item", axis=0, tiled=True)
    n_slots = owners * CAP
    tile_slot = jnp.clip(tile_slot, 0, n_slots - 1).astype(jnp.int32)
    slot_order = jnp.arange(tile_slots, dtype=jnp.int32)
    seen_before = (tile_slot[None, :] == tile_slot[:, None]) & (slot_order[None, :] < slot_order[:, None])
    first_touch = jnp.logical_not(jnp.any(seen_before, axis=1)).astype(jnp.int32)
    user_total, send_rows = tile_work(
        jnp.clip(users_here, 0, slab_blocks.shape[0] - 1).astype(jnp.int32),
        jnp.clip(items_here, 0, span_blocks - 1).astype(jnp.int32),
        tile_slot,
        first_touch,
        tile_count[0].astype(jnp.int32),
        slab_blocks,
        whole_table.reshape(span_blocks, tile_edge, factor_width),
        ratings[0],
        n_slots,
    )
    send_rows = send_rows.reshape(owners, CAP * tile_edge, factor_width)
    arrived, arrived_ids = (
        lax.all_to_all(send_rows, "item", split_axis=0, concat_axis=0, tiled=True),
        lax.all_to_all(request, "item", split_axis=0, concat_axis=0, tiled=True),
    )
    factors_new, mean_new, square_new = owner_update(
        arrived_ids.reshape(-1).astype(jnp.int32),
        arrived.reshape(owners * CAP, tile_edge, factor_width),
        item_factors,
        item_mean,
        item_square,
    )
    user_gradient = lax.psum_scatter(
        user_total.reshape(-1, factor_width),
        "band",
        scatter_dimension=0,
        tiled=True,
    )
    return (user_gradient, factors_new, mean_new, square_new)


def solution(mesh):
    in_specs = (
        P(("band", "item"), None),
        P(("band", "item"), None),
        P(("band", "item"), None),
        P(("band", "item"), None),
        P("band", "item", None, None),
        P("band", "item"),
        P("band", "item"),
        P("band", "item"),
    )
    out_specs = (
        P(("band", "item"), None),
        P(("band", "item"), None),
        P(("band", "item"), None),
        P(("band", "item"), None),
    )
    return jax.shard_map(body, mesh=mesh, in_specs=in_specs, out_specs=out_specs, check_vma=False)
```
